256 devices in a mesh: section: 2 (over core), tok: 32 (over z, y), rep: 4 (over x).
Axes of the slice: x: 4, y: 4, z: 8, core: 2. Of those that a mesh axis runs over, the one named last changes fastest.
Arguments:
- inputs: bfloat16 [2, 4096, 1024], P(None, 'tok')
- segment_ids: int32 [2, 4096], replicated, may hold values from 0 to 7, as said below
- picks: int32 [2, 4096, 2], P(None, 'tok'), may hold values from 0 to 15, all different within a row; in each aligned block of 128 rows (0 to 127, 128 to 255, ..., all dimensions but the last counted through in order) at most 20 rows name the same one
- page_table: int32 [2, 32], replicated, may hold values from 0 to 31, each once within a row
- norm_gains: float32 [2, 2, 1024], P('section'), may hold values from 0.1 to 1.9
- attn_qkv: bfloat16 [2, 1024, 3, 1024], P('section', None, None, 'rep')
- attn_out: bfloat16 [2, 1024, 1024], P('section', 'rep'), may hold values from -0.1875 to 0.1875
- router: bfloat16 [2, 1024, 16], P('section')
- expert_in: bfloat16 [2, 32, 1024, 2, 1408], P('section', 'tok', None, None, 'rep'), may hold values from -0.1875 to 0.1875
- expert_out: bfloat16 [2, 32, 1408, 1024], P('section', 'tok', 'rep')
Outputs:
- layer_out: bfloat16 [2, 2, 4096, 1024], P('section', None, 'tok')
- kv_pages: bfloat16 [2, 2, 32, 128, 2, 1024], P('section', None, 'tok', None, None, 'rep')
The draws below stay inside these ranges and needn't reach their ends.
Inputs may be any that keep to these rules, and one draw needn't show every extreme that they name: `picks`: within the tokens of one index of tok in one micro-batch, at most 20 tokens pick one expert, and some expert is picked by exactly 20. `segment_ids`: ids never fall along a micro-batch; every prompt has at least one token, a prompt spans at most 2048 tokens and one spans exactly 2048. `page_table`: each row is a permutation.
All inputs are finite; a program needn't handle non-finite values.
Results may differ from the reference program's by a relative error of at most 0.034.
Values may be sent and summed in bfloat16 or wider, within the bound.
No kernel may reach another device: no remote copies, remote signals or barrier semaphores. Data moves between devices by JAX's collectives and lax.ppermute only.
A program may use at most 128 MiB of HBM per device.

```python
import math
import jax
import jax.numpy as jnp
import numpy as np
from jax import lax

D = 1024
HEADS = 16
HEAD_DIM = 64
FF = 2816
EXPERTS = 16
TOP = 2
PAGE = 128
MB = 2
NPROMPT = 8
TOK_DEV = 128
LAYERS = 2
TOKENS = 4096
LONGEST = 2048
CAP = 20
SPLIT = 2
PAGES_ALL = 32
N_TOK = 32
N_REP = 4


def prompt_layout(key):
    base_key = jax.random.fold_in(key, 9173)
    remaining = TOKENS - LONGEST

    def one_batch(batch_key):
        first_key, second_key = jax.random.split(batch_key, 2)
        long_place = jax.random.randint(first_key, (), 0, NPROMPT).astype(jnp.int32)
        shuffled = jax.random.permutation(second_key, remaining - 1)[:NPROMPT - 2].astype(jnp.int32) + 1
        cut_points = jnp.sort(shuffled)
        boundaries = jnp.concatenate([jnp.zeros((1,), jnp.int32), cut_points, jnp.full((1,), remaining, jnp.int32)])
        short_lengths = boundaries[1:] - boundaries[:-1]
        prompt_ids = jnp.arange(NPROMPT, dtype=jnp.int32)
        source_ids = jnp.where(prompt_ids > long_place, prompt_ids - 1, prompt_ids)
        source_ids = jnp.clip(source_ids, 0, NPROMPT - 2)
        lengths = jnp.where(prompt_ids == long_place, LONGEST, jnp.take(short_lengths, source_ids))
        return (lengths.astype(jnp.int32), long_place)
    micro_keys = jax.random.split(base_key, MB)
    return jax.vmap(one_batch)(micro_keys)


def draw_segment_ids(key, part):
    lengths, long_place = prompt_layout(key)
    prompt_ends = jnp.cumsum(lengths, axis=1).astype(jnp.int32)
    positions = jnp.arange(TOKENS, dtype=jnp.int32)
    passed = (positions[None, :, None] >= prompt_ends[:, None, :]).astype(jnp.int32)
    return jnp.sum(passed, axis=2).astype(jnp.int32)


def draw_inputs(key, part):
    noise = jax.random.normal(jax.random.fold_in(key, 311), (MB, TOKENS, D), jnp.float32)
    noise = jnp.clip(noise, -6.0, 6.0)
    return noise.astype(jnp.bfloat16)


def draw_attn_qkv(key, part):
    first = jax.random.fold_in(key, 0)
    base = jax.random.normal(first, (LAYERS, D, 3, D), jnp.float32) * D ** (-0.5)
    return base.astype(jnp.bfloat16)


def draw_router(key, part):
    factor = 1.5
    return (jax.random.normal(key, (LAYERS, D, EXPERTS), jnp.float32) * factor * D ** (-0.5)).astype(jnp.bfloat16)


def draw_expert_out(key, part):
    first, second = jax.random.split(key, 2)
    base = jnp.clip(jax.random.normal(first, (LAYERS, EXPERTS * SPLIT, FF // SPLIT, D), jnp.float32), -6.0, 6.0)
    base = base * FF ** (-0.5)
    expert_scale = jnp.exp(jax.random.uniform(second, (LAYERS, EXPERTS, 1, 1, 1), jnp.float32, -1.5, 1.5))
    expert_scale = jnp.broadcast_to(expert_scale, (LAYERS, EXPERTS, SPLIT, 1, 1)).reshape(LAYERS, EXPERTS * SPLIT, 1, 1)
    return (base * expert_scale).astype(jnp.bfloat16)


def block_levels(rng, shape, cuts, low, top_value):
    gain = 1.0
    for axis_at, blocks in cuts:
        draws = jax.random.uniform(jax.random.fold_in(jax.random.fold_in(rng, 6), axis_at), (blocks,), jnp.float32, low / len(cuts), top_value / len(cuts))
        gain = gain * jnp.repeat(jnp.exp(draws), shape[axis_at] // blocks).reshape((-1,) + (1,) * (len(shape) - 1 - axis_at))
    return gain


def deal_out(stream_key, own, number, rows, count, top, most, skew):
    ranking = jax.random.permutation(stream_key, count)
    crowded, ordinary = load_shares(count, rows * top, most, skew, True), load_shares(count, rows * top, most, skew, False)
    places = jnp.arange(count)

    def named(tallies, rotation):
        used = int((tallies > 0).sum())
        fixed = max(1, used // 4)
        moved = fixed + (places - fixed + rotation * (used - fixed)) % max(1, count - fixed)
        return jnp.zeros((count,), jnp.int32).at[ranking[jnp.where(places < fixed, places, moved)]].set(jnp.asarray(tallies, jnp.int32))

    tallies = jnp.where(number % 4 == 0, named(crowded, number // 4), named(ordinary, number - number // 4 - 1))
    mixed = jax.random.permutation(jax.random.fold_in(own, 3), count)
    source_of, receiver = mixed[0:count // 2 * 2:2], mixed[1:count // 2 * 2:2]
    slack = jnp.minimum(tallies[source_of] - 1, most - tallies[receiver]) // 2
    slack = jnp.where((source_of == ranking[0]) | (receiver == ranking[0]) | (tallies[receiver] == 0), 0, jnp.maximum(slack, 0))
    moved = jax.random.randint(jax.random.fold_in(own, 4), (count // 2,), 0, 1 << 20) % (slack + 1)
    tallies = tallies.at[source_of].add(-moved).at[receiver].add(moved)
    items = jnp.searchsorted(jnp.cumsum(tallies), jnp.arange(rows * top), side="right").astype(jnp.int32)
    table = items.reshape(top, rows).T
    table = table[jax.random.permutation(jax.random.fold_in(own, 1), rows)]
    rotation = jax.random.randint(jax.random.fold_in(own, 2), (rows, 1), 0, top)
    return jnp.take_along_axis(table, (jnp.arange(top)[None, :] + rotation) % top, axis=1)


def load_shares(count, total, reach, lean, full):
    loads = [(1 << 20) // math.isqrt(rank ** lean) + 1 for rank in range(1, count + 1)]
    largest = reach if full else min(reach, max(-(-total // count), total * loads[0] // sum(loads)))
    least = 1 if total - largest >= count - 1 else 0
    counts, rest = [largest] + [least] * (count - 1), total - largest - least * (count - 1)
    while rest > 0:
        movable = [i for i in range(1, count) if counts[i] < largest] or [i for i in range(1, count) if counts[i] < reach]
        whole, left = sum([loads[i] for i in movable]), rest
        for i in movable:
            more = min(reach - counts[i], max(1, left * loads[i] // whole), rest)
            counts[i] = counts[i] + more
            rest = rest - more
    return np.array(counts)


def centred(rng, dims, scale, reach, cuts=(), kind=jnp.bfloat16):
    values = jax.random.normal(rng, dims, jnp.float32) * scale
    if len(cuts) > 0:
        values = block_levels(rng, dims, cuts, -0.22, 0.18) * values
    return jnp.clip(values, min=-reach, max=reach).astype(kind)


def setup_inputs(seed: int = 0) -> dict:
    splits = jax.random.split(jax.random.key(seed), 11)
    inputs = draw_inputs(jax.random.fold_in(splits[10], 71), 0)
    segment_ids = draw_segment_ids(jax.random.fold_in(splits[10], 71), 0)
    picks_keys = jax.random.split(jax.random.fold_in(splits[2], 1), MB * TOKENS // TOK_DEV)
    picks_turns = jax.random.permutation(jax.random.fold_in(splits[2], 3), MB * TOKENS // TOK_DEV)
    picks = jax.vmap(lambda own, number: deal_out(jax.random.fold_in(splits[2], 2), own, number, TOK_DEV, EXPERTS, TOP, CAP, 2))(picks_keys, picks_turns).reshape((MB, TOKENS, TOP))
    page_table = jax.vmap(lambda own: jax.random.permutation(own, PAGES_ALL))(jax.random.split(splits[3], MB)).reshape((MB, PAGES_ALL)).astype(jnp.int32)
    norm_gains = jnp.clip(1.0 + 0.18 * jax.random.normal(splits[4], (LAYERS, 2, D), jnp.float32), 0.1, 1.9)
    attn_qkv = draw_attn_qkv(jax.random.fold_in(splits[10], 71), 0)
    attn_out = centred(splits[6], (LAYERS, D, D), D ** -0.5, 0.1875, ((0, 2), (1, 4)))
    router = draw_router(jax.random.fold_in(splits[10], 71), 0)
    expert_in = centred(splits[8], (LAYERS, EXPERTS * SPLIT, D, 2, FF // SPLIT), D ** -0.5, 0.1875, ((0, 2), (1, 32), (4, 4)))
    expert_out = draw_expert_out(jax.random.fold_in(splits[10], 71), 0)
    return {"inputs": inputs, "segment_ids": segment_ids, "picks": picks, "page_table": page_table, "norm_gains": norm_gains, "attn_qkv": attn_qkv, "attn_out": attn_out, "router": router, "expert_in": expert_in, "expert_out": expert_out}


def rms_scale(values, gains):
    return values * lax.rsqrt(lax.optimization_barrier(jnp.mean(values * values, axis=-1, keepdims=True)) + 1e-06) * gains.astype(jnp.float32)

def attention_part(normed, w_qkv, seg_row):
    projected = jnp.dot(normed, w_qkv.reshape(D, 3 * D), preferred_element_type=jnp.float32).astype(jnp.bfloat16)
    split_heads = projected.reshape(TOKENS, 3, HEADS, HEAD_DIM)
    queries = split_heads[:, 0].transpose(1, 0, 2)
    keys_all = split_heads[:, 1].transpose(1, 0, 2)
    values_all = split_heads[:, 2].transpose(1, 0, 2)
    positions = jnp.arange(TOKENS, dtype=jnp.int32)
    visible = (seg_row[:, None] == seg_row[None, :]) & (positions[:, None] >= positions[None, :])

    def one_head(operands):
        head_q, head_k, head_v = operands
        scores = jnp.dot(head_q, head_k.T, preferred_element_type=jnp.float32) * HEAD_DIM ** (-0.5)
        scores = jnp.where(visible, scores, -jnp.inf)
        weights = jax.nn.softmax(scores, axis=-1)
        return jnp.dot(weights, head_v.astype(jnp.float32), precision=lax.Precision.HIGHEST)
    context = lax.map(one_head, (queries, keys_all, values_all))
    context = context.transpose(1, 0, 2).reshape(TOKENS, D).astype(jnp.bfloat16)
    return (context, projected.reshape(TOKENS, 3, D)[:, 1:])

def expert_part(normed_mid, picks_row, w_router, w_in, w_down):
    logits = jnp.dot(normed_mid, w_router, preferred_element_type=jnp.float32)
    expert_ids = jnp.arange(EXPERTS, dtype=jnp.int32)
    chosen = (picks_row[:, :, None] == expert_ids[None, None, :]).astype(jnp.int32)
    picked_logit = lax.optimization_barrier(jnp.sum(chosen.astype(jnp.float32) * logits[:, None, :], axis=-1))
    top_logit = lax.optimization_barrier(jnp.max(picked_logit, axis=-1, keepdims=True))
    raised = jnp.exp(picked_logit - top_logit)
    gate_vals = raised / lax.optimization_barrier(jnp.sum(raised, axis=-1, keepdims=True))
    chosen_dev = chosen.reshape(N_TOK, TOK_DEV, TOP, EXPERTS)
    ordered = chosen_dev.transpose(0, 2, 1, 3).reshape(N_TOK, TOP * TOK_DEV, EXPERTS)
    slot_of = lax.optimization_barrier(jnp.sum((jnp.cumsum(ordered, axis=1) - 1) * ordered, axis=-1))
    expert_flat = picks_row.reshape(N_TOK, TOK_DEV, TOP).transpose(0, 2, 1).reshape(N_TOK, TOP * TOK_DEV)
    flat_slot = (expert_flat * CAP + slot_of).astype(jnp.int32)
    dev_rows = normed_mid.reshape(N_TOK, TOK_DEV, D)
    rows_twice = jnp.concatenate([dev_rows] * TOP, axis=1)
    dev_index = jnp.arange(N_TOK, dtype=jnp.int32)[:, None]
    buffers = jnp.zeros((N_TOK, EXPERTS * CAP, D), jnp.bfloat16).at[dev_index, flat_slot].set(rows_twice)
    per_expert = buffers.reshape(N_TOK, EXPERTS, CAP, D).transpose(1, 0, 2, 3).reshape(EXPERTS, N_TOK * CAP, D)
    piece_width = FF // SPLIT
    share_width = piece_width // N_REP
    w_in_e = w_in.reshape(EXPERTS, SPLIT, D, 2, piece_width)
    w_down_e = w_down.reshape(EXPERTS, SPLIT, N_REP, share_width, D)

    def one_expert(operands):
        rows, w_first, w_second = operands
        act = jnp.einsum('rd,sdgf->rsgf', rows.astype(jnp.float32), w_first.astype(jnp.float32))
        hidden = (jax.nn.gelu(act[:, :, 0]) * act[:, :, 1]).astype(jnp.bfloat16)
        hidden = hidden.reshape(rows.shape[0], SPLIT, N_REP, share_width)
        share_out = jnp.einsum('rsqf,sqfd->rsqd', hidden.astype(jnp.float32), w_second.astype(jnp.float32))
        share_out = lax.optimization_barrier(share_out.astype(jnp.bfloat16))
        return lax.optimization_barrier(jnp.sum(share_out.astype(jnp.float32), axis=(1, 2)))
    outs = lax.map(one_expert, (per_expert, w_in_e, w_down_e))
    outs = outs.reshape(EXPERTS, N_TOK, CAP, D).transpose(1, 0, 2, 3).reshape(N_TOK, EXPERTS * CAP, D)
    gathered = jnp.take_along_axis(outs, flat_slot[:, :, None], axis=1).reshape(N_TOK, TOP, TOK_DEV, D)
    gates_dev = gate_vals.reshape(N_TOK, TOK_DEV, TOP).transpose(0, 2, 1)
    combined = lax.optimization_barrier(jnp.sum(gates_dev[:, :, :, None] * gathered, axis=1))
    return combined.reshape(TOKENS, D)

def one_layer(hidden_in, seg_row, picks_row, table_row, gains, w_qkv, w_out, w_router, w_in, w_down):
    resid = hidden_in.astype(jnp.float32)
    normed = rms_scale(resid, gains[0]).astype(jnp.bfloat16)
    context, keys_vals = attention_part(normed, w_qkv, seg_row)
    mid = resid + jnp.dot(context, w_out, preferred_element_type=jnp.float32)
    normed_mid = rms_scale(mid, gains[1]).astype(jnp.bfloat16)
    result = (mid + expert_part(normed_mid, picks_row, w_router, w_in, w_down)).astype(jnp.bfloat16)
    blocks = keys_vals.reshape(PAGES_ALL, PAGE, 2, D)
    pages = jnp.zeros((PAGES_ALL, PAGE, 2, D), jnp.bfloat16).at[table_row].set(blocks)
    return (result, pages)

def reference(inputs, segment_ids, picks, page_table, norm_gains, attn_qkv, attn_out, router, expert_in, expert_out):
    layer_outs = [[None] * MB for layer in range(LAYERS)]
    layer_pages = [[None] * MB for layer in range(LAYERS)]
    for micro in range(MB):
        hidden = inputs[micro]
        for layer in range(LAYERS):
            hidden, pages = one_layer(hidden, segment_ids[micro], picks[micro], page_table[micro], norm_gains[layer], attn_qkv[layer], attn_out[layer], router[layer], expert_in[layer], expert_out[layer])
            layer_outs[layer][micro] = hidden
            layer_pages[layer][micro] = pages
    out_stack = jnp.stack([jnp.stack(row) for row in layer_outs])
    page_stack = jnp.stack([jnp.stack(row) for row in layer_pages])
    return (out_stack, page_stack)
```

```python
import jax
import jax.numpy as jnp
from jax import lax
from jax.sharding import PartitionSpec as P

HEAD_DIM = 64
TOP = 2
PAGE = 128
CAP = 20


NEG_FILL = -1e30


def shifted(value, axis, steps):
    count = lax.axis_size(axis)
    first, last = (max(0, -steps), min(count, count - steps))
    return lax.ppermute(value, axis, [(source, source + steps) for source in range(first, last)])


def rms_scale(values, gains):
    return values * lax.rsqrt(jnp.mean(values * values, axis=-1, keepdims=True) + 1e-06) * gains


def attend(carry, queries, keys_vals, seg_query, pos_query, seg_key, pos_key):
    run_max, run_sum, run_acc = carry
    heads_here = run_acc.shape[0]
    head_size = run_acc.shape[2]
    rows_key = keys_vals.shape[0]
    key_part = keys_vals[:, 0].reshape(rows_key, heads_here, head_size)
    val_part = keys_vals[:, 1].reshape(rows_key, heads_here, head_size).astype(jnp.float32)
    scores = jnp.einsum(
        "thd,nhd->htn", queries, key_part, preferred_element_type=jnp.float32
    ) * head_size ** (-0.5)
    visible = (seg_query[:, None] == seg_key[None, :]) & (pos_query[:, None] >= pos_key[None, :])
    masked = jnp.where(visible[None], scores, NEG_FILL)
    new_max = jnp.maximum(run_max, jnp.max(masked, axis=-1))
    weights = jnp.where(visible[None], jnp.exp(masked - new_max[..., None]), 0.0)
    decay = jnp.exp(run_max - new_max)
    run_sum = run_sum * decay + jnp.sum(weights, axis=-1)
    run_acc = run_acc * decay[..., None] + jnp.einsum(
        "htn,nhd->htd", weights, val_part, precision=lax.Precision.HIGHEST
    )
    return (new_max, run_sum, run_acc)


def place_pages(pages, keys_vals, table_row, tok_index):
    rows_here = keys_vals.shape[0]
    blocks_dev = pages.shape[0]
    page_rows = pages.shape[1]
    block_ids = jnp.arange(table_row.shape[0], dtype=jnp.int32)
    wanted = tok_index * blocks_dev + 0
    source = jnp.sum(jnp.where(table_row == wanted, block_ids, 0))
    offset = source * page_rows
    inside = (offset >= 0) & (offset + page_rows <= rows_here)
    block = lax.dynamic_slice_in_dim(
        keys_vals, jnp.clip(offset, 0, rows_here - page_rows), page_rows, 0
    )
    updated = [jnp.where(inside, block, pages[0])]
    return jnp.stack(updated)


def one_layer(
    layer_in, seg_all, table_row, pick_rows, gains, w_qkv, w_out, w_router, w_in, w_down
):
    tok_index = lax.axis_index("tok")
    tok_count = lax.axis_size("tok")
    tok_rows = layer_in.shape[0]
    width = layer_in.shape[1]
    col_width = w_qkv.shape[1] // 3
    head_count = col_width // HEAD_DIM
    experts_all = w_router.shape[1]
    local_pieces = w_in.shape[0]
    split_count = local_pieces * tok_count // experts_all
    blocks_dev = tok_rows // PAGE
    row_ids = jnp.arange(tok_rows, dtype=jnp.int32)
    pos_query = tok_index * tok_rows + row_ids
    seg_query = lax.dynamic_slice_in_dim(seg_all, tok_index * tok_rows, tok_rows)
    resid = layer_in.astype(jnp.float32)
    normed = rms_scale(resid, gains[0]).astype(jnp.bfloat16)
    projected = jnp.dot(normed, w_qkv, preferred_element_type=jnp.float32).astype(jnp.bfloat16)
    projected = projected.reshape(tok_rows, 3, col_width)
    queries = projected[:, 0].reshape(tok_rows, head_count, HEAD_DIM)
    keys_vals = projected[:, 1:]
    soft_init = (
        jnp.full((head_count, tok_rows), NEG_FILL, jnp.float32),
        jnp.zeros((head_count, tok_rows), jnp.float32),
        jnp.zeros((head_count, tok_rows, HEAD_DIM), jnp.float32),
    )
    empty_pages = jnp.zeros((blocks_dev, PAGE, 2, col_width), jnp.bfloat16)
    piece = lax.all_gather(keys_vals, "tok", axis=0, tiled=True)
    rows_key = piece.shape[0]
    step_rows = 1024
    while rows_key % step_rows != 0:
        step_rows = step_rows // 2
    turns = rows_key // step_rows

    def key_block(index, soft_now):
        start = index * step_rows
        block = lax.dynamic_slice_in_dim(piece, start, step_rows, 0)
        seg_key = lax.dynamic_slice_in_dim(seg_all, start, step_rows)
        pos_key = start + jnp.arange(step_rows, dtype=jnp.int32)
        return attend(soft_now, queries, block, seg_query, pos_query, seg_key, pos_key)

    soft_next = lax.fori_loop(0, turns, key_block, soft_init)
    pages = place_pages(empty_pages, piece, table_row, tok_index)
    run_max, run_sum, run_acc = soft_next
    context = (
        (run_acc / run_sum[..., None])
        .transpose(1, 0, 2)
        .reshape(tok_rows, col_width)
        .astype(jnp.bfloat16)
    )
    attn_part = jnp.dot(context, w_out, preferred_element_type=jnp.float32)
    mid = resid + lax.psum(attn_part, "rep")
    normed_mid = rms_scale(mid, gains[1]).astype(jnp.bfloat16)
    logits = jnp.dot(normed_mid, w_router, preferred_element_type=jnp.float32)
    expert_ids = jnp.arange(experts_all, dtype=jnp.int32)
    chosen = (pick_rows[:, :, None] == expert_ids[None, None, :]).astype(jnp.int32)
    picked_logit = jnp.sum(chosen.astype(jnp.float32) * logits[:, None, :], axis=-1)
    top_logit = jnp.max(picked_logit, axis=-1, keepdims=True)
    raised = jnp.exp(picked_logit - top_logit)
    gate_vals = raised / jnp.sum(raised, axis=-1, keepdims=True)
    ordered = chosen.transpose(1, 0, 2).reshape(TOP * tok_rows, experts_all)
    slot_of = jnp.sum((jnp.cumsum(ordered, axis=0) - 1) * ordered, axis=-1)
    flat_slot = pick_rows.T.reshape(TOP * tok_rows) * CAP + slot_of
    slot_ids = jnp.arange(experts_all * CAP, dtype=jnp.int32)
    hits = (flat_slot[:, None] == slot_ids[None, :]).astype(jnp.int32)
    hits = jnp.sum(hits.reshape(TOP, tok_rows, experts_all * CAP), axis=0).astype(jnp.bfloat16)
    dispatch = lax.dot_general(
        hits, normed_mid, (((0,), (0,)), ((), ())), preferred_element_type=jnp.float32
    ).astype(jnp.bfloat16)
    copies = jnp.broadcast_to(
        dispatch.reshape(experts_all, 1, CAP, width), (experts_all, split_count, CAP, width)
    )
    copies = copies.reshape(tok_count, local_pieces, CAP, width)
    act = jnp.einsum(
        "secd,edgf->secgf",
        lax.all_to_all(copies, "tok", split_axis=0, concat_axis=0, tiled=True),
        w_in,
        preferred_element_type=jnp.float32,
    )
    hidden = (jax.nn.gelu(act[..., 0, :]) * act[..., 1, :]).astype(jnp.bfloat16)
    returned = lax.all_to_all(
        jnp.einsum("secf,efd->secd", hidden, w_down, preferred_element_type=jnp.float32).astype(
            jnp.bfloat16
        ),
        "tok",
        split_axis=0,
        concat_axis=0,
        tiled=True,
    )
    summed = jnp.sum(
        returned.reshape(experts_all, split_count, CAP, width).astype(jnp.float32), axis=1
    )
    summed = summed.reshape(experts_all * CAP, width)
    gathered = jnp.take(summed, flat_slot, axis=0).reshape(TOP, tok_rows, width)
    expert_local = jnp.sum(gate_vals.T[:, :, None] * gathered, axis=0)
    expert_total = lax.psum(expert_local, "rep")
    layer_result = (mid + expert_total).astype(jnp.bfloat16)
    return layer_result, pages


def per_device(
    inputs,
    segment_ids,
    picks,
    page_table,
    norm_gains,
    attn_qkv,
    attn_out,
    router,
    expert_in,
    expert_out,
):
    section_index = lax.axis_index("section")
    is_first = section_index == 0
    width = inputs.shape[2]
    own = (
        norm_gains[0],
        attn_qkv[0].reshape(width, -1),
        attn_out[0],
        router[0],
        expert_in[0],
        expert_out[0],
    )
    swap = [(0, 1), (1, 0)]
    other = tuple(lax.ppermute(w, "section", swap) for w in own)
    weights_of = [
        tuple(jnp.where(is_first, a, b) for a, b in zip(own, other)),
        tuple(jnp.where(is_first, b, a) for a, b in zip(own, other)),
    ]
    micro = section_index
    hidden = lax.dynamic_index_in_dim(inputs, micro, 0, keepdims=False)
    seg_all = lax.dynamic_index_in_dim(segment_ids, micro, 0, keepdims=False)
    table_row = lax.dynamic_index_in_dim(page_table, micro, 0, keepdims=False)
    pick_rows = lax.dynamic_index_in_dim(picks, micro, 0, keepdims=False)
    results = []
    for layer in range(2):
        hidden, pages = one_layer(hidden, seg_all, table_row, pick_rows, *weights_of[layer])
        results.append((hidden, pages))
    (res0, pages0), (res1, pages1) = results
    got0 = lax.ppermute(res0, "section", [(1, 0)])
    gotp0 = lax.ppermute(pages0, "section", [(1, 0)])
    got1 = lax.ppermute(res1, "section", [(0, 1)])
    gotp1 = lax.ppermute(pages1, "section", [(0, 1)])
    outputs = jnp.where(is_first, jnp.stack([res0, got0]), jnp.stack([got1, res1]))
    page_out = jnp.where(is_first, jnp.stack([pages0, gotp0]), jnp.stack([gotp1, pages1]))
    return (outputs[None], page_out[None])


def solution(mesh):
    return jax.shard_map(
        per_device,
        mesh=mesh,
        in_specs=(
            P(None, "tok", None),
            P(),
            P(None, "tok", None),
            P(),
            P("section", None, None),
            P("section", None, None, "rep"),
            P("section", "rep", None),
            P("section", None, None),
            P("section", "tok", None, None, "rep"),
            P("section", "tok", "rep", None),
        ),
        out_specs=(P("section", None, "tok", None), P("section", None, "tok", None, None, "rep")),
        check_vma=False,
    )
```

```python
import jax
import jax.numpy as jnp
from jax import lax
from jax.sharding import PartitionSpec as P

HEAD_DIM = 64
TOP = 2
PAGE = 128
CAP = 20


NEG_FILL = -1e30


def shifted(value, axis, steps):
    count = lax.axis_size(axis)
    first, last = (max(0, -steps), min(count, count - steps))
    return lax.ppermute(value, axis, [(source, source + steps) for source in range(first, last)])


def rms_scale(values, gains):
    return values * lax.rsqrt(jnp.mean(values * values, axis=-1, keepdims=True) + 1e-06) * gains


def rep_sum(values):
    count = lax.axis_size("rep")
    total = values.astype(jnp.bfloat16)
    stride = 1
    while stride < count:
        pairs = [(index, index ^ stride) for index in range(count)]
        partner = lax.ppermute(total, "rep", pairs)
        summed = total.astype(jnp.float32) + partner.astype(jnp.float32)
        stride = stride * 2
        total = summed.astype(jnp.bfloat16) if stride < count else summed
    return total


def attend(carry, queries, keys_vals, seg_query, pos_query, seg_key, pos_key):
    run_max, run_sum, run_acc = carry
    heads_here = run_acc.shape[0]
    head_size = run_acc.shape[2]
    rows_key = keys_vals.shape[0]
    key_part = keys_vals[:, 0].reshape(rows_key, heads_here, head_size)
    val_part = keys_vals[:, 1].reshape(rows_key, heads_here, head_size).astype(jnp.float32)
    scores = jnp.einsum(
        "thd,nhd->htn", queries, key_part, preferred_element_type=jnp.float32
    ) * head_size ** (-0.5)
    visible = (seg_query[:, None] == seg_key[None, :]) & (pos_query[:, None] >= pos_key[None, :])
    masked = jnp.where(visible[None], scores, NEG_FILL)
    new_max = jnp.maximum(run_max, jnp.max(masked, axis=-1))
    weights = jnp.where(visible[None], jnp.exp(masked - new_max[..., None]), 0.0)
    decay = jnp.exp(run_max - new_max)
    run_sum = run_sum * decay + jnp.sum(weights, axis=-1)
    run_acc = run_acc * decay[..., None] + jnp.einsum(
        "htn,nhd->htd", weights, val_part, precision=lax.Precision.HIGHEST
    )
    return (new_max, run_sum, run_acc)


def place_pages(pages, keys_vals, table_row, tok_index):
    rows_here = keys_vals.shape[0]
    blocks_dev = pages.shape[0]
    page_rows = pages.shape[1]
    block_ids = jnp.arange(table_row.shape[0], dtype=jnp.int32)
    wanted = tok_index * blocks_dev + 0
    source = jnp.sum(jnp.where(table_row == wanted, block_ids, 0))
    offset = source * page_rows
    inside = (offset >= 0) & (offset + page_rows <= rows_here)
    block = lax.dynamic_slice_in_dim(
        keys_vals, jnp.clip(offset, 0, rows_here - page_rows), page_rows, 0
    )
    updated = [jnp.where(inside, block, pages[0])]
    return jnp.stack(updated)


def one_layer(
    layer_in, seg_all, table_row, pick_rows, gains, w_qkv, w_out, w_router, w_in, w_down
):
    tok_index = lax.axis_index("tok")
    tok_count = lax.axis_size("tok")
    tok_rows = layer_in.shape[0]
    width = layer_in.shape[1]
    col_width = w_qkv.shape[1] // 3
    head_count = col_width // HEAD_DIM
    experts_all = w_router.shape[1]
    local_pieces = w_in.shape[0]
    split_count = local_pieces * tok_count // experts_all
    blocks_dev = tok_rows // PAGE
    row_ids = jnp.arange(tok_rows, dtype=jnp.int32)
    pos_query = tok_index * tok_rows + row_ids
    seg_query = lax.dynamic_slice_in_dim(seg_all, tok_index * tok_rows, tok_rows)
    resid = layer_in.astype(jnp.float32)
    normed = rms_scale(resid, gains[0]).astype(jnp.bfloat16)
    projected = jnp.dot(normed, w_qkv, preferred_element_type=jnp.float32).astype(jnp.bfloat16)
    projected = projected.reshape(tok_rows, 3, col_width)
    queries = projected[:, 0].reshape(tok_rows, head_count, HEAD_DIM)
    keys_vals = projected[:, 1:]
    soft_init = (
        jnp.full((head_count, tok_rows), NEG_FILL, jnp.float32),
        jnp.zeros((head_count, tok_rows), jnp.float32),
        jnp.zeros((head_count, tok_rows, HEAD_DIM), jnp.float32),
    )
    empty_pages = jnp.zeros((blocks_dev, PAGE, 2, col_width), jnp.bfloat16)
    piece = lax.all_gather(keys_vals, "tok", axis=0, tiled=True)
    rows_key = piece.shape[0]
    step_rows = 1024
    while rows_key % step_rows != 0:
        step_rows = step_rows // 2
    turns = rows_key // step_rows

    def key_block(index, soft_now):
        start = index * step_rows
        block = lax.dynamic_slice_in_dim(piece, start, step_rows, 0)
        seg_key = lax.dynamic_slice_in_dim(seg_all, start, step_rows)
        pos_key = start + jnp.arange(step_rows, dtype=jnp.int32)
        return attend(soft_now, queries, block, seg_query, pos_query, seg_key, pos_key)

    soft_next = lax.fori_loop(0, turns, key_block, soft_init)
    pages = place_pages(empty_pages, piece, table_row, tok_index)
    run_max, run_sum, run_acc = soft_next
    context = (
        (run_acc / run_sum[..., None])
        .transpose(1, 0, 2)
        .reshape(tok_rows, col_width)
        .astype(jnp.bfloat16)
    )
    attn_part = jnp.dot(context, w_out, preferred_element_type=jnp.float32)
    mid = resid + rep_sum(attn_part)
    normed_mid = rms_scale(mid, gains[1]).astype(jnp.bfloat16)
    logits = jnp.dot(normed_mid, w_router, preferred_element_type=jnp.float32)
    expert_ids = jnp.arange(experts_all, dtype=jnp.int32)
    chosen = (pick_rows[:, :, None] == expert_ids[None, None, :]).astype(jnp.int32)
    picked_logit = jnp.sum(chosen.astype(jnp.float32) * logits[:, None, :], axis=-1)
    top_logit = jnp.max(picked_logit, axis=-1, keepdims=True)
    raised = jnp.exp(picked_logit - top_logit)
    gate_vals = raised / jnp.sum(raised, axis=-1, keepdims=True)
    ordered = chosen.transpose(1, 0, 2).reshape(TOP * tok_rows, experts_all)
    slot_of = jnp.sum((jnp.cumsum(ordered, axis=0) - 1) * ordered, axis=-1)
    flat_slot = pick_rows.T.reshape(TOP * tok_rows) * CAP + slot_of
    slot_ids = jnp.arange(experts_all * CAP, dtype=jnp.int32)
    hits = (flat_slot[:, None] == slot_ids[None, :]).astype(jnp.int32)
    hits = jnp.sum(hits.reshape(TOP, tok_rows, experts_all * CAP), axis=0).astype(jnp.bfloat16)
    dispatch = lax.dot_general(
        hits, normed_mid, (((0,), (0,)), ((), ())), preferred_element_type=jnp.float32
    ).astype(jnp.bfloat16)
    copies = jnp.broadcast_to(
        dispatch.reshape(experts_all, 1, CAP, width), (experts_all, split_count, CAP, width)
    )
    copies = copies.reshape(tok_count, local_pieces, CAP, width)
    act = jnp.einsum(
        "secd,edgf->secgf",
        lax.all_to_all(copies, "tok", split_axis=0, concat_axis=0, tiled=True),
        w_in,
        preferred_element_type=jnp.float32,
    )
    hidden = (jax.nn.gelu(act[..., 0, :]) * act[..., 1, :]).astype(jnp.bfloat16)
    returned = lax.all_to_all(
        jnp.einsum("secf,efd->secd", hidden, w_down, preferred_element_type=jnp.float32).astype(
            jnp.bfloat16
        ),
        "tok",
        split_axis=0,
        concat_axis=0,
        tiled=True,
    )
    summed = jnp.sum(
        returned.reshape(experts_all, split_count, CAP, width).astype(jnp.float32), axis=1
    )
    summed = summed.reshape(experts_all * CAP, width)
    gathered = jnp.take(summed, flat_slot, axis=0).reshape(TOP, tok_rows, width)
    expert_local = jnp.sum(gate_vals.T[:, :, None] * gathered, axis=0)
    expert_total = rep_sum(expert_local)
    layer_result = (mid + expert_total).astype(jnp.bfloat16)
    return layer_result, pages


def per_device(
    inputs,
    segment_ids,
    picks,
    page_table,
    norm_gains,
    attn_qkv,
    attn_out,
    router,
    expert_in,
    expert_out,
):
    section_index = lax.axis_index("section")
    is_first = section_index == 0
    width = inputs.shape[2]
    own = (
        norm_gains[0],
        attn_qkv[0].reshape(width, -1),
        attn_out[0],
        router[0],
        expert_in[0],
        expert_out[0],
    )
    swap = [(0, 1), (1, 0)]
    other = tuple(lax.ppermute(w, "section", swap) for w in own)
    weights_of = [
        tuple(jnp.where(is_first, a, b) for a, b in zip(own, other)),
        tuple(jnp.where(is_first, b, a) for a, b in zip(own, other)),
    ]
    micro = section_index
    hidden = lax.dynamic_index_in_dim(inputs, micro, 0, keepdims=False)
    seg_all = lax.dynamic_index_in_dim(segment_ids, micro, 0, keepdims=False)
    table_row = lax.dynamic_index_in_dim(page_table, micro, 0, keepdims=False)
    pick_rows = lax.dynamic_index_in_dim(picks, micro, 0, keepdims=False)
    results = []
    for layer in range(2):
        hidden, pages = one_layer(hidden, seg_all, table_row, pick_rows, *weights_of[layer])
        results.append((hidden, pages))
    (res0, pages0), (res1, pages1) = results
    got0 = lax.ppermute(res0, "section", [(1, 0)])
    gotp0 = lax.ppermute(pages0, "section", [(1, 0)])
    got1 = lax.ppermute(res1, "section", [(0, 1)])
    gotp1 = lax.ppermute(pages1, "section", [(0, 1)])
    outputs = jnp.where(is_first, jnp.stack([res0, got0]), jnp.stack([got1, res1]))
    page_out = jnp.where(is_first, jnp.stack([pages0, gotp0]), jnp.stack([gotp1, pages1]))
    return (outputs[None], page_out[None])


def solution(mesh):
    return jax.shard_map(
        per_device,
        mesh=mesh,
        in_specs=(
            P(None, "tok", None),
            P(),
            P(None, "tok", None),
            P(),
            P("section", None, None),
            P("section", None, None, "rep"),
            P("section", "rep", None),
            P("section", None, None),
            P("section", "tok", None, None, "rep"),
            P("section", "tok", "rep", None),
        ),
        out_specs=(P("section", None, "tok", None), P("section", None, "tok", None, None, "rep")),
        check_vma=False,
    )
```

```python
import jax
import jax.numpy as jnp
from jax import lax
from jax.sharding import PartitionSpec as P

HEAD_DIM = 64
TOP = 2
PAGE = 128
CAP = 20


NEG_FILL = -1e30


def shifted(value, axis, steps):
    count = lax.axis_size(axis)
    first, last = (max(0, -steps), min(count, count - steps))
    return lax.ppermute(value, axis, [(source, source + steps) for source in range(first, last)])


def rms_scale(values, gains):
    return values * lax.rsqrt(jnp.mean(values * values, axis=-1, keepdims=True) + 1e-06) * gains


def rep_sum(values):
    count = lax.axis_size("rep")
    total = values.astype(jnp.bfloat16)
    stride = 1
    while stride < count:
        pairs = [(index, index ^ stride) for index in range(count)]
        partner = lax.ppermute(total, "rep", pairs)
        summed = total.astype(jnp.float32) + partner.astype(jnp.float32)
        stride = stride * 2
        total = summed.astype(jnp.bfloat16) if stride < count else summed
    return total


def ring_gather(block):
    tok_count = lax.axis_size("tok")
    inner = 4 if tok_count % 4 == 0 else 1
    outer = tok_count // inner
    tok_index = lax.axis_index("tok")
    outer_at = tok_index // inner
    inner_at = tok_index % inner

    def moved(value, size, stride, steps):
        pairs = []
        for source in range(tok_count):
            high, low = source // inner, source % inner
            if stride == 1:
                low = (low + steps) % size
            else:
                high = (high + steps) % size
            pairs.append((source, high * inner + low))
        return lax.ppermute(value, "tok", pairs)

    def ring(value, size, stride):
        ahead = [value]
        behind = []
        fwd = value
        back = value
        for step in range(size // 2):
            fwd = moved(fwd, size, stride, -1)
            ahead.append(fwd)
            if len(ahead) + len(behind) == size:
                break
            back = moved(back, size, stride, 1)
            behind.append(back)
        return jnp.stack(ahead + behind[::-1])

    group = ring(block, inner, 1) if inner > 1 else block[None]
    every = ring(group, outer, inner).reshape((tok_count,) + block.shape)
    ids = jnp.arange(tok_count, dtype=jnp.int32)
    rel = ((ids // inner - outer_at) % outer) * inner + (ids % inner - inner_at) % inner
    return jnp.take(every, rel, axis=0).reshape((tok_count * block.shape[0],) + block.shape[1:])


def attend(carry, queries, keys_vals, seg_query, pos_query, seg_key, pos_key):
    run_max, run_sum, run_acc = carry
    heads_here = run_acc.shape[0]
    head_size = run_acc.shape[2]
    rows_key = keys_vals.shape[0]
    key_part = keys_vals[:, 0].reshape(rows_key, heads_here, head_size)
    val_part = keys_vals[:, 1].reshape(rows_key, heads_here, head_size).astype(jnp.float32)
    scores = jnp.einsum(
        "thd,nhd->htn", queries, key_part, preferred_element_type=jnp.float32
    ) * head_size ** (-0.5)
    visible = (seg_query[:, None] == seg_key[None, :]) & (pos_query[:, None] >= pos_key[None, :])
    masked = jnp.where(visible[None], scores, NEG_FILL)
    new_max = jnp.maximum(run_max, jnp.max(masked, axis=-1))
    weights = jnp.where(visible[None], jnp.exp(masked - new_max[..., None]), 0.0)
    decay = jnp.exp(run_max - new_max)
    run_sum = run_sum * decay + jnp.sum(weights, axis=-1)
    run_acc = run_acc * decay[..., None] + jnp.einsum(
        "htn,nhd->htd", weights, val_part, precision=lax.Precision.HIGHEST
    )
    return (new_max, run_sum, run_acc)


def place_pages(pages, keys_vals, table_row, tok_index):
    rows_here = keys_vals.shape[0]
    blocks_dev = pages.shape[0]
    page_rows = pages.shape[1]
    block_ids = jnp.arange(table_row.shape[0], dtype=jnp.int32)
    wanted = tok_index * blocks_dev + 0
    source = jnp.sum(jnp.where(table_row == wanted, block_ids, 0))
    offset = source * page_rows
    inside = (offset >= 0) & (offset + page_rows <= rows_here)
    block = lax.dynamic_slice_in_dim(
        keys_vals, jnp.clip(offset, 0, rows_here - page_rows), page_rows, 0
    )
    updated = [jnp.where(inside, block, pages[0])]
    return jnp.stack(updated)


def one_layer(
    layer_in, seg_all, table_row, pick_rows, gains, w_qkv, w_out, w_router, w_in, w_down
):
    tok_index = lax.axis_index("tok")
    tok_count = lax.axis_size("tok")
    tok_rows = layer_in.shape[0]
    width = layer_in.shape[1]
    col_width = w_qkv.shape[1] // 3
    head_count = col_width // HEAD_DIM
    experts_all = w_router.shape[1]
    local_pieces = w_in.shape[0]
    split_count = local_pieces * tok_count // experts_all
    blocks_dev = tok_rows // PAGE
    row_ids = jnp.arange(tok_rows, dtype=jnp.int32)
    pos_query = tok_index * tok_rows + row_ids
    seg_query = lax.dynamic_slice_in_dim(seg_all, tok_index * tok_rows, tok_rows)
    resid = layer_in.astype(jnp.float32)
    normed = rms_scale(resid, gains[0]).astype(jnp.bfloat16)
    projected = jnp.dot(normed, w_qkv, preferred_element_type=jnp.float32).astype(jnp.bfloat16)
    projected = projected.reshape(tok_rows, 3, col_width)
    queries = projected[:, 0].reshape(tok_rows, head_count, HEAD_DIM)
    keys_vals = projected[:, 1:]
    soft_init = (
        jnp.full((head_count, tok_rows), NEG_FILL, jnp.float32),
        jnp.zeros((head_count, tok_rows), jnp.float32),
        jnp.zeros((head_count, tok_rows, HEAD_DIM), jnp.float32),
    )
    empty_pages = jnp.zeros((blocks_dev, PAGE, 2, col_width), jnp.bfloat16)
    piece = ring_gather(keys_vals)
    rows_key = piece.shape[0]
    step_rows = 1024
    while rows_key % step_rows != 0:
        step_rows = step_rows // 2
    turns = rows_key // step_rows

    def key_block(index, soft_now):
        start = index * step_rows
        block = lax.dynamic_slice_in_dim(piece, start, step_rows, 0)
        seg_key = lax.dynamic_slice_in_dim(seg_all, start, step_rows)
        pos_key = start + jnp.arange(step_rows, dtype=jnp.int32)
        return attend(soft_now, queries, block, seg_query, pos_query, seg_key, pos_key)

    soft_next = lax.fori_loop(0, turns, key_block, soft_init)
    pages = place_pages(empty_pages, piece, table_row, tok_index)
    run_max, run_sum, run_acc = soft_next
    context = (
        (run_acc / run_sum[..., None])
        .transpose(1, 0, 2)
        .reshape(tok_rows, col_width)
        .astype(jnp.bfloat16)
    )
    attn_part = jnp.dot(context, w_out, preferred_element_type=jnp.float32)
    mid = resid + rep_sum(attn_part)
    normed_mid = rms_scale(mid, gains[1]).astype(jnp.bfloat16)
    logits = jnp.dot(normed_mid, w_router, preferred_element_type=jnp.float32)
    expert_ids = jnp.arange(experts_all, dtype=jnp.int32)
    chosen = (pick_rows[:, :, None] == expert_ids[None, None, :]).astype(jnp.int32)
    picked_logit = jnp.sum(chosen.astype(jnp.float32) * logits[:, None, :], axis=-1)
    top_logit = jnp.max(picked_logit, axis=-1, keepdims=True)
    raised = jnp.exp(picked_logit - top_logit)
    gate_vals = raised / jnp.sum(raised, axis=-1, keepdims=True)
    ordered = chosen.transpose(1, 0, 2).reshape(TOP * tok_rows, experts_all)
    slot_of = jnp.sum((jnp.cumsum(ordered, axis=0) - 1) * ordered, axis=-1)
    flat_slot = pick_rows.T.reshape(TOP * tok_rows) * CAP + slot_of
    slot_ids = jnp.arange(experts_all * CAP, dtype=jnp.int32)
    hits = (flat_slot[:, None] == slot_ids[None, :]).astype(jnp.int32)
    hits = jnp.sum(hits.reshape(TOP, tok_rows, experts_all * CAP), axis=0).astype(jnp.bfloat16)
    dispatch = lax.dot_general(
        hits, normed_mid, (((0,), (0,)), ((), ())), preferred_element_type=jnp.float32
    ).astype(jnp.bfloat16)
    copies = jnp.broadcast_to(
        dispatch.reshape(experts_all, 1, CAP, width), (experts_all, split_count, CAP, width)
    )
    copies = copies.reshape(tok_count, local_pieces, CAP, width)
    act = jnp.einsum(
        "secd,edgf->secgf",
        lax.all_to_all(copies, "tok", split_axis=0, concat_axis=0, tiled=True),
        w_in,
        preferred_element_type=jnp.float32,
    )
    hidden = (jax.nn.gelu(act[..., 0, :]) * act[..., 1, :]).astype(jnp.bfloat16)
    returned = lax.all_to_all(
        jnp.einsum("secf,efd->secd", hidden, w_down, preferred_element_type=jnp.float32).astype(
            jnp.bfloat16
        ),
        "tok",
        split_axis=0,
        concat_axis=0,
        tiled=True,
    )
    summed = jnp.sum(
        returned.reshape(experts_all, split_count, CAP, width).astype(jnp.float32), axis=1
    )
    summed = summed.reshape(experts_all * CAP, width)
    gathered = jnp.take(summed, flat_slot, axis=0).reshape(TOP, tok_rows, width)
    expert_local = jnp.sum(gate_vals.T[:, :, None] * gathered, axis=0)
    expert_total = rep_sum(expert_local)
    layer_result = (mid + expert_total).astype(jnp.bfloat16)
    return layer_result, pages


def per_device(
    inputs,
    segment_ids,
    picks,
    page_table,
    norm_gains,
    attn_qkv,
    attn_out,
    router,
    expert_in,
    expert_out,
):
    section_index = lax.axis_index("section")
    is_first = section_index == 0
    width = inputs.shape[2]
    own = (
        norm_gains[0],
        attn_qkv[0].reshape(width, -1),
        attn_out[0],
        router[0],
        expert_in[0],
        expert_out[0],
    )
    swap = [(0, 1), (1, 0)]
    other = tuple(lax.ppermute(w, "section", swap) for w in own)
    weights_of = [
        tuple(jnp.where(is_first, a, b) for a, b in zip(own, other)),
        tuple(jnp.where(is_first, b, a) for a, b in zip(own, other)),
    ]
    micro = section_index
    hidden = lax.dynamic_index_in_dim(inputs, micro, 0, keepdims=False)
    seg_all = lax.dynamic_index_in_dim(segment_ids, micro, 0, keepdims=False)
    table_row = lax.dynamic_index_in_dim(page_table, micro, 0, keepdims=False)
    pick_rows = lax.dynamic_index_in_dim(picks, micro, 0, keepdims=False)
    results = []
    for layer in range(2):
        hidden, pages = one_layer(hidden, seg_all, table_row, pick_rows, *weights_of[layer])
        results.append((hidden, pages))
    (res0, pages0), (res1, pages1) = results
    got0 = lax.ppermute(res0, "section", [(1, 0)])
    gotp0 = lax.ppermute(pages0, "section", [(1, 0)])
    got1 = lax.ppermute(res1, "section", [(0, 1)])
    gotp1 = lax.ppermute(pages1, "section", [(0, 1)])
    outputs = jnp.where(is_first, jnp.stack([res0, got0]), jnp.stack([got1, res1]))
    page_out = jnp.where(is_first, jnp.stack([pages0, gotp0]), jnp.stack([gotp1, pages1]))
    return (outputs[None], page_out[None])


def solution(mesh):
    return jax.shard_map(
        per_device,
        mesh=mesh,
        in_specs=(
            P(None, "tok", None),
            P(),
            P(None, "tok", None),
            P(),
            P("section", None, None),
            P("section", None, None, "rep"),
            P("section", "rep", None),
            P("section", None, None),
            P("section", "tok", None, None, "rep"),
            P("section", "tok", "rep", None),
        ),
        out_specs=(P("section", None, "tok", None), P("section", None, "tok", None, None, "rep")),
        check_vma=False,
    )
```

```python
import jax
import jax.numpy as jnp
from jax import lax
from jax.sharding import PartitionSpec as P

HEAD_DIM = 64
TOP = 2
PAGE = 128
CAP = 20


NEG_FILL = -1e30


def shifted(value, axis, steps):
    count = lax.axis_size(axis)
    first, last = (max(0, -steps), min(count, count - steps))
    return lax.ppermute(value, axis, [(source, source + steps) for source in range(first, last)])


def rms_scale(values, gains):
    return values * lax.rsqrt(jnp.mean(values * values, axis=-1, keepdims=True) + 1e-06) * gains


def rep_sum(values):
    count = lax.axis_size("rep")
    total = values.astype(jnp.bfloat16)
    stride = 1
    while stride < count:
        pairs = [(index, index ^ stride) for index in range(count)]
        partner = lax.ppermute(total, "rep", pairs)
        summed = total.astype(jnp.float32) + partner.astype(jnp.float32)
        stride = stride * 2
        total = summed.astype(jnp.bfloat16) if stride < count else summed
    return total


def attend(carry, queries, keys_vals, seg_query, pos_query, seg_key, pos_key):
    run_max, run_sum, run_acc = carry
    heads_here = run_acc.shape[0]
    head_size = run_acc.shape[2]
    rows_key = keys_vals.shape[0]
    key_part = keys_vals[:, 0].reshape(rows_key, heads_here, head_size)
    val_part = keys_vals[:, 1].reshape(rows_key, heads_here, head_size).astype(jnp.float32)
    scores = jnp.einsum(
        "thd,nhd->htn", queries, key_part, preferred_element_type=jnp.float32
    ) * head_size ** (-0.5)
    visible = (seg_query[:, None] == seg_key[None, :]) & (pos_query[:, None] >= pos_key[None, :])
    masked = jnp.where(visible[None], scores, NEG_FILL)
    new_max = jnp.maximum(run_max, jnp.max(masked, axis=-1))
    weights = jnp.where(visible[None], jnp.exp(masked - new_max[..., None]), 0.0)
    decay = jnp.exp(run_max - new_max)
    run_sum = run_sum * decay + jnp.sum(weights, axis=-1)
    run_acc = run_acc * decay[..., None] + jnp.einsum(
        "htn,nhd->htd", weights, val_part, precision=lax.Precision.HIGHEST
    )
    return (new_max, run_sum, run_acc)


def place_pages(pages, keys_vals, table_row, tok_index):
    rows_here = keys_vals.shape[0]
    blocks_dev = pages.shape[0]
    page_rows = pages.shape[1]
    block_ids = jnp.arange(table_row.shape[0], dtype=jnp.int32)
    wanted = tok_index * blocks_dev + 0
    source = jnp.sum(jnp.where(table_row == wanted, block_ids, 0))
    offset = source * page_rows
    inside = (offset >= 0) & (offset + page_rows <= rows_here)
    block = lax.dynamic_slice_in_dim(
        keys_vals, jnp.clip(offset, 0, rows_here - page_rows), page_rows, 0
    )
    updated = [jnp.where(inside, block, pages[0])]
    return jnp.stack(updated)


def one_layer(
    layer_in, seg_all, table_row, pick_rows, gains, w_qkv, w_out, w_router, w_in, w_down
):
    tok_index = lax.axis_index("tok")
    tok_count = lax.axis_size("tok")
    tok_rows = layer_in.shape[0]
    width = layer_in.shape[1]
    col_width = w_qkv.shape[1] // 3
    head_count = col_width // HEAD_DIM
    experts_all = w_router.shape[1]
    local_pieces = w_in.shape[0]
    split_count = local_pieces * tok_count // experts_all
    blocks_dev = tok_rows // PAGE
    row_ids = jnp.arange(tok_rows, dtype=jnp.int32)
    pos_query = tok_index * tok_rows + row_ids
    seg_query = lax.dynamic_slice_in_dim(seg_all, tok_index * tok_rows, tok_rows)
    resid = layer_in.astype(jnp.float32)
    normed = rms_scale(resid, gains[0]).astype(jnp.bfloat16)
    projected = jnp.dot(normed, w_qkv, preferred_element_type=jnp.float32).astype(jnp.bfloat16)
    projected = projected.reshape(tok_rows, 3, col_width)
    queries = projected[:, 0].reshape(tok_rows, head_count, HEAD_DIM)
    keys_vals = projected[:, 1:]
    soft_init = (
        jnp.full((head_count, tok_rows), NEG_FILL, jnp.float32),
        jnp.zeros((head_count, tok_rows), jnp.float32),
        jnp.zeros((head_count, tok_rows, HEAD_DIM), jnp.float32),
    )
    empty_pages = jnp.zeros((blocks_dev, PAGE, 2, col_width), jnp.bfloat16)
    piece = lax.all_gather(keys_vals, "tok", axis=0, tiled=True)
    rows_key = piece.shape[0]
    step_rows = 512
    while rows_key % step_rows != 0:
        step_rows = step_rows // 2
    seg_start = jnp.sum((seg_all < seg_query[0]).astype(jnp.int32))
    first_turn = seg_start // step_rows
    last_turn = (tok_index * tok_rows + tok_rows - 1) // step_rows

    def key_block(index, soft_now):
        start = index * step_rows
        block = lax.dynamic_slice_in_dim(piece, start, step_rows, 0)
        seg_key = lax.dynamic_slice_in_dim(seg_all, start, step_rows)
        pos_key = start + jnp.arange(step_rows, dtype=jnp.int32)
        return attend(soft_now, queries, block, seg_query, pos_query, seg_key, pos_key)

    soft_next = lax.fori_loop(first_turn, last_turn + 1, key_block, soft_init)
    pages = place_pages(empty_pages, piece, table_row, tok_index)
    run_max, run_sum, run_acc = soft_next
    context = (
        (run_acc / run_sum[..., None])
        .transpose(1, 0, 2)
        .reshape(tok_rows, col_width)
        .astype(jnp.bfloat16)
    )
    attn_part = jnp.dot(context, w_out, preferred_element_type=jnp.float32)
    mid = resid + rep_sum(attn_part)
    normed_mid = rms_scale(mid, gains[1]).astype(jnp.bfloat16)
    logits = jnp.dot(normed_mid, w_router, preferred_element_type=jnp.float32)
    expert_ids = jnp.arange(experts_all, dtype=jnp.int32)
    chosen = (pick_rows[:, :, None] == expert_ids[None, None, :]).astype(jnp.int32)
    picked_logit = jnp.sum(chosen.astype(jnp.float32) * logits[:, None, :], axis=-1)
    top_logit = jnp.max(picked_logit, axis=-1, keepdims=True)
    raised = jnp.exp(picked_logit - top_logit)
    gate_vals = raised / jnp.sum(raised, axis=-1, keepdims=True)
    ordered = chosen.transpose(1, 0, 2).reshape(TOP * tok_rows, experts_all)
    slot_of = jnp.sum((jnp.cumsum(ordered, axis=0) - 1) * ordered, axis=-1)
    flat_slot = pick_rows.T.reshape(TOP * tok_rows) * CAP + slot_of
    slot_ids = jnp.arange(experts_all * CAP, dtype=jnp.int32)
    hits = (flat_slot[:, None] == slot_ids[None, :]).astype(jnp.int32)
    hits = jnp.sum(hits.reshape(TOP, tok_rows, experts_all * CAP), axis=0).astype(jnp.bfloat16)
    dispatch = lax.dot_general(
        hits, normed_mid, (((0,), (0,)), ((), ())), preferred_element_type=jnp.float32
    ).astype(jnp.bfloat16)
    copies = jnp.broadcast_to(
        dispatch.reshape(experts_all, 1, CAP, width), (experts_all, split_count, CAP, width)
    )
    copies = copies.reshape(tok_count, local_pieces, CAP, width)
    act = jnp.einsum(
        "secd,edgf->secgf",
        lax.all_to_all(copies, "tok", split_axis=0, concat_axis=0, tiled=True),
        w_in,
        preferred_element_type=jnp.float32,
    )
    hidden = (jax.nn.gelu(act[..., 0, :]) * act[..., 1, :]).astype(jnp.bfloat16)
    returned = lax.all_to_all(
        jnp.einsum("secf,efd->secd", hidden, w_down, preferred_element_type=jnp.float32).astype(
            jnp.bfloat16
        ),
        "tok",
        split_axis=0,
        concat_axis=0,
        tiled=True,
    )
    summed = jnp.sum(
        returned.reshape(experts_all, split_count, CAP, width).astype(jnp.float32), axis=1
    )
    summed = summed.reshape(experts_all * CAP, width)
    gathered = jnp.take(summed, flat_slot, axis=0).reshape(TOP, tok_rows, width)
    expert_local = jnp.sum(gate_vals.T[:, :, None] * gathered, axis=0)
    expert_total = rep_sum(expert_local)
    layer_result = (mid + expert_total).astype(jnp.bfloat16)
    return layer_result, pages


def per_device(
    inputs,
    segment_ids,
    picks,
    page_table,
    norm_gains,
    attn_qkv,
    attn_out,
    router,
    expert_in,
    expert_out,
):
    section_index = lax.axis_index("section")
    is_first = section_index == 0
    width = inputs.shape[2]
    own = (
        norm_gains[0],
        attn_qkv[0].reshape(width, -1),
        attn_out[0],
        router[0],
        expert_in[0],
        expert_out[0],
    )
    swap = [(0, 1), (1, 0)]
    other = tuple(lax.ppermute(w, "section", swap) for w in own)
    weights_of = [
        tuple(jnp.where(is_first, a, b) for a, b in zip(own, other)),
        tuple(jnp.where(is_first, b, a) for a, b in zip(own, other)),
    ]
    micro = section_index
    hidden = lax.dynamic_index_in_dim(inputs, micro, 0, keepdims=False)
    seg_all = lax.dynamic_index_in_dim(segment_ids, micro, 0, keepdims=False)
    table_row = lax.dynamic_index_in_dim(page_table, micro, 0, keepdims=False)
    pick_rows = lax.dynamic_index_in_dim(picks, micro, 0, keepdims=False)
    results = []
    for layer in range(2):
        hidden, pages = one_layer(hidden, seg_all, table_row, pick_rows, *weights_of[layer])
        results.append((hidden, pages))
    (res0, pages0), (res1, pages1) = results
    got0 = lax.ppermute(res0, "section", [(1, 0)])
    gotp0 = lax.ppermute(pages0, "section", [(1, 0)])
    got1 = lax.ppermute(res1, "section", [(0, 1)])
    gotp1 = lax.ppermute(pages1, "section", [(0, 1)])
    outputs = jnp.where(is_first, jnp.stack([res0, got0]), jnp.stack([got1, res1]))
    page_out = jnp.where(is_first, jnp.stack([pages0, gotp0]), jnp.stack([gotp1, pages1]))
    return (outputs[None], page_out[None])


def solution(mesh):
    return jax.shard_map(
        per_device,
        mesh=mesh,
        in_specs=(
            P(None, "tok", None),
            P(),
            P(None, "tok", None),
            P(),
            P("section", None, None),
            P("section", None, None, "rep"),
            P("section", "rep", None),
            P("section", None, None),
            P("section", "tok", None, None, "rep"),
            P("section", "tok", "rep", None),
        ),
        out_specs=(P("section", None, "tok", None), P("section", None, "tok", None, None, "rep")),
        check_vma=False,
    )
```

```python
import jax
import jax.numpy as jnp
from jax import lax
from jax.sharding import Mesh, PartitionSpec as P

HEAD_DIM = 64
TOP = 2
PAGE = 128
CAP = 20


NEG_FILL = -1e30


def shifted(value, axis, steps):
    count = lax.axis_size(axis)
    first, last = (max(0, -steps), min(count, count - steps))
    return lax.ppermute(value, axis, [(source, source + steps) for source in range(first, last)])


def rms_scale(values, gains):
    return values * lax.rsqrt(jnp.mean(values * values, axis=-1, keepdims=True) + 1e-06) * gains


def tok_place():
    return lax.axis_index("tz") * lax.axis_size("tp") + lax.axis_index("tp")


def tok_size():
    return lax.axis_size("tz") * lax.axis_size("tp")


def rep_sum(values):
    count = lax.axis_size("rep")
    total = values.astype(jnp.bfloat16)
    stride = 1
    while stride < count:
        pairs = [(index, index ^ stride) for index in range(count)]
        partner = lax.ppermute(total, "rep", pairs)
        summed = total.astype(jnp.float32) + partner.astype(jnp.float32)
        stride = stride * 2
        total = summed.astype(jnp.bfloat16) if stride < count else summed
    return total


def attend(carry, queries, keys_vals, seg_query, pos_query, seg_key, pos_key):
    run_max, run_sum, run_acc = carry
    heads_here = run_acc.shape[0]
    head_size = run_acc.shape[2]
    rows_key = keys_vals.shape[0]
    key_part = keys_vals[:, 0].reshape(rows_key, heads_here, head_size)
    val_part = keys_vals[:, 1].reshape(rows_key, heads_here, head_size).astype(jnp.float32)
    scores = jnp.einsum(
        "thd,nhd->htn", queries, key_part, preferred_element_type=jnp.float32
    ) * head_size ** (-0.5)
    visible = (seg_query[:, None] == seg_key[None, :]) & (pos_query[:, None] >= pos_key[None, :])
    masked = jnp.where(visible[None], scores, NEG_FILL)
    new_max = jnp.maximum(run_max, jnp.max(masked, axis=-1))
    weights = jnp.where(visible[None], jnp.exp(masked - new_max[..., None]), 0.0)
    decay = jnp.exp(run_max - new_max)
    run_sum = run_sum * decay + jnp.sum(weights, axis=-1)
    run_acc = run_acc * decay[..., None] + jnp.einsum(
        "htn,nhd->htd", weights, val_part, precision=lax.Precision.HIGHEST
    )
    return (new_max, run_sum, run_acc)


def place_pages(pages, keys_vals, table_row, tok_index):
    rows_here = keys_vals.shape[0]
    blocks_dev = pages.shape[0]
    page_rows = pages.shape[1]
    block_ids = jnp.arange(table_row.shape[0], dtype=jnp.int32)
    wanted = tok_index * blocks_dev + 0
    source = jnp.sum(jnp.where(table_row == wanted, block_ids, 0))
    offset = source * page_rows
    inside = (offset >= 0) & (offset + page_rows <= rows_here)
    block = lax.dynamic_slice_in_dim(
        keys_vals, jnp.clip(offset, 0, rows_here - page_rows), page_rows, 0
    )
    updated = [jnp.where(inside, block, pages[0])]
    return jnp.stack(updated)


def one_layer(
    layer_in, seg_all, table_row, pick_rows, gains, w_qkv, w_out, w_router, w_in, w_down
):
    tok_index = tok_place()
    tok_count = tok_size()
    tok_rows = layer_in.shape[0]
    width = layer_in.shape[1]
    col_width = w_qkv.shape[1] // 3
    head_count = col_width // HEAD_DIM
    experts_all = w_router.shape[1]
    local_pieces = w_in.shape[0]
    split_count = local_pieces * tok_count // experts_all
    blocks_dev = tok_rows // PAGE
    row_ids = jnp.arange(tok_rows, dtype=jnp.int32)
    pos_query = tok_index * tok_rows + row_ids
    seg_query = lax.dynamic_slice_in_dim(seg_all, tok_index * tok_rows, tok_rows)
    resid = layer_in.astype(jnp.float32)
    normed = rms_scale(resid, gains[0]).astype(jnp.bfloat16)
    projected = jnp.dot(normed, w_qkv, preferred_element_type=jnp.float32).astype(jnp.bfloat16)
    projected = projected.reshape(tok_rows, 3, col_width)
    queries = projected[:, 0].reshape(tok_rows, head_count, HEAD_DIM)
    keys_vals = projected[:, 1:]
    soft_init = (
        jnp.full((head_count, tok_rows), NEG_FILL, jnp.float32),
        jnp.zeros((head_count, tok_rows), jnp.float32),
        jnp.zeros((head_count, tok_rows, HEAD_DIM), jnp.float32),
    )
    empty_pages = jnp.zeros((blocks_dev, PAGE, 2, col_width), jnp.bfloat16)
    piece = lax.all_gather(keys_vals, ("tz", "tp"), axis=0, tiled=True)
    rows_key = piece.shape[0]
    step_rows = 512
    while rows_key % step_rows != 0:
        step_rows = step_rows // 2
    seg_start = jnp.sum((seg_all < seg_query[0]).astype(jnp.int32))
    first_turn = seg_start // step_rows
    last_turn = (tok_index * tok_rows + tok_rows - 1) // step_rows

    def key_block(index, soft_now):
        start = index * step_rows
        block = lax.dynamic_slice_in_dim(piece, start, step_rows, 0)
        seg_key = lax.dynamic_slice_in_dim(seg_all, start, step_rows)
        pos_key = start + jnp.arange(step_rows, dtype=jnp.int32)
        return attend(soft_now, queries, block, seg_query, pos_query, seg_key, pos_key)

    soft_next = lax.fori_loop(first_turn, last_turn + 1, key_block, soft_init)
    pages = place_pages(empty_pages, piece, table_row, tok_index)
    run_max, run_sum, run_acc = soft_next
    context = (
        (run_acc / run_sum[..., None])
        .transpose(1, 0, 2)
        .reshape(tok_rows, col_width)
        .astype(jnp.bfloat16)
    )
    attn_part = jnp.dot(context, w_out, preferred_element_type=jnp.float32)
    mid = resid + rep_sum(attn_part)
    normed_mid = rms_scale(mid, gains[1]).astype(jnp.bfloat16)
    logits = jnp.dot(normed_mid, w_router, preferred_element_type=jnp.float32)
    expert_ids = jnp.arange(experts_all, dtype=jnp.int32)
    chosen = (pick_rows[:, :, None] == expert_ids[None, None, :]).astype(jnp.int32)
    picked_logit = jnp.sum(chosen.astype(jnp.float32) * logits[:, None, :], axis=-1)
    top_logit = jnp.max(picked_logit, axis=-1, keepdims=True)
    raised = jnp.exp(picked_logit - top_logit)
    gate_vals = raised / jnp.sum(raised, axis=-1, keepdims=True)
    ordered = chosen.transpose(1, 0, 2).reshape(TOP * tok_rows, experts_all)
    slot_of = jnp.sum((jnp.cumsum(ordered, axis=0) - 1) * ordered, axis=-1)
    flat_slot = pick_rows.T.reshape(TOP * tok_rows) * CAP + slot_of
    slot_ids = jnp.arange(experts_all * CAP, dtype=jnp.int32)
    hits = (flat_slot[:, None] == slot_ids[None, :]).astype(jnp.int32)
    hits = jnp.sum(hits.reshape(TOP, tok_rows, experts_all * CAP), axis=0).astype(jnp.bfloat16)
    dispatch = lax.dot_general(
        hits, normed_mid, (((0,), (0,)), ((), ())), preferred_element_type=jnp.float32
    ).astype(jnp.bfloat16)
    pair_swap = [(0, 1), (1, 0)]
    own_rows = lax.all_to_all(
        dispatch.reshape(experts_all, CAP, width), "tz", split_axis=0, concat_axis=0, tiled=True
    )
    pair_rows = lax.ppermute(own_rows, "tp", pair_swap)
    rows_all = jnp.stack([own_rows, pair_rows]).reshape(-1, width)
    act = jnp.einsum("rd,dgf->rgf", rows_all, w_in[0], preferred_element_type=jnp.float32)
    hidden = (jax.nn.gelu(act[:, 0, :]) * act[:, 1, :]).astype(jnp.bfloat16)
    share_out = jnp.dot(hidden, w_down[0], preferred_element_type=jnp.float32).astype(jnp.bfloat16)
    share_out = share_out.reshape(2, experts_all, CAP, width)
    pair_out = lax.ppermute(share_out[1], "tp", pair_swap)
    halves = (share_out[0].astype(jnp.float32) + pair_out.astype(jnp.float32)).astype(jnp.bfloat16)
    returned = lax.all_to_all(halves, "tz", split_axis=0, concat_axis=0, tiled=True)
    summed = returned.astype(jnp.float32).reshape(experts_all * CAP, width)
    gathered = jnp.take(summed, flat_slot, axis=0).reshape(TOP, tok_rows, width)
    expert_local = jnp.sum(gate_vals.T[:, :, None] * gathered, axis=0)
    expert_total = rep_sum(expert_local)
    layer_result = (mid + expert_total).astype(jnp.bfloat16)
    return layer_result, pages


def per_device(
    inputs,
    segment_ids,
    picks,
    page_table,
    norm_gains,
    attn_qkv,
    attn_out,
    router,
    expert_in,
    expert_out,
):
    section_index = lax.axis_index("section")
    is_first = section_index == 0
    width = inputs.shape[2]
    own = (
        norm_gains[0],
        attn_qkv[0].reshape(width, -1),
        attn_out[0],
        router[0],
        expert_in[0],
        expert_out[0],
    )
    swap = [(0, 1), (1, 0)]
    other = tuple(lax.ppermute(w, "section", swap) for w in own)
    weights_of = [
        tuple(jnp.where(is_first, a, b) for a, b in zip(own, other)),
        tuple(jnp.where(is_first, b, a) for a, b in zip(own, other)),
    ]
    micro = section_index
    hidden = lax.dynamic_index_in_dim(inputs, micro, 0, keepdims=False)
    seg_all = lax.dynamic_index_in_dim(segment_ids, micro, 0, keepdims=False)
    table_row = lax.dynamic_index_in_dim(page_table, micro, 0, keepdims=False)
    pick_rows = lax.dynamic_index_in_dim(picks, micro, 0, keepdims=False)
    results = []
    for layer in range(2):
        hidden, pages = one_layer(hidden, seg_all, table_row, pick_rows, *weights_of[layer])
        results.append((hidden, pages))
    (res0, pages0), (res1, pages1) = results
    got0 = lax.ppermute(res0, "section", [(1, 0)])
    gotp0 = lax.ppermute(pages0, "section", [(1, 0)])
    got1 = lax.ppermute(res1, "section", [(0, 1)])
    gotp1 = lax.ppermute(pages1, "section", [(0, 1)])
    outputs = jnp.where(is_first, jnp.stack([res0, got0]), jnp.stack([got1, res1]))
    page_out = jnp.where(is_first, jnp.stack([pages0, gotp0]), jnp.stack([gotp1, pages1]))
    return (outputs[None], page_out[None])


def solution(mesh):
    sizes = mesh.shape
    pair = 2
    grid = mesh.devices.reshape(sizes["section"], sizes["tok"] // pair, pair, sizes["rep"])
    split_mesh = Mesh(grid, ("section", "tz", "tp", "rep"))
    tok = ("tz", "tp")
    return jax.shard_map(
        per_device,
        mesh=split_mesh,
        in_specs=(
            P(None, tok, None),
            P(),
            P(None, tok, None),
            P(),
            P("section", None, None),
            P("section", None, None, "rep"),
            P("section", "rep", None),
            P("section", None, None),
            P("section", tok, None, None, "rep"),
            P("section", tok, "rep", None),
        ),
        out_specs=(P("section", None, tok, None), P("section", None, tok, None, None, "rep")),
        check_vma=False,
    )
```

```python
import jax
import jax.numpy as jnp
from jax import lax
from jax.sharding import Mesh, PartitionSpec as P

HEAD_DIM = 64
TOP = 2
PAGE = 128
CAP = 20
LONGEST = 2048


NEG_FILL = -1e30


def shifted(value, axis, steps):
    count = lax.axis_size(axis)
    first, last = (max(0, -steps), min(count, count - steps))
    return lax.ppermute(value, axis, [(source, source + steps) for source in range(first, last)])


def rms_scale(values, gains):
    return values * lax.rsqrt(jnp.mean(values * values, axis=-1, keepdims=True) + 1e-06) * gains


def tok_place():
    return lax.axis_index("tz") * lax.axis_size("tp") + lax.axis_index("tp")


def tok_size():
    return lax.axis_size("tz") * lax.axis_size("tp")


def rep_sum(values):
    count = lax.axis_size("rep")
    total = values.astype(jnp.bfloat16)
    stride = 1
    while stride < count:
        pairs = [(index, index ^ stride) for index in range(count)]
        partner = lax.ppermute(total, "rep", pairs)
        summed = total.astype(jnp.float32) + partner.astype(jnp.float32)
        stride = stride * 2
        total = summed.astype(jnp.bfloat16) if stride < count else summed
    return total


def attend(carry, queries, keys_vals, seg_query, pos_query, seg_key, pos_key):
    run_max, run_sum, run_acc = carry
    heads_here = run_acc.shape[0]
    head_size = run_acc.shape[2]
    rows_key = keys_vals.shape[0]
    key_part = keys_vals[:, 0].reshape(rows_key, heads_here, head_size)
    val_part = keys_vals[:, 1].reshape(rows_key, heads_here, head_size).astype(jnp.float32)
    scores = jnp.einsum(
        "thd,nhd->htn", queries, key_part, preferred_element_type=jnp.float32
    ) * head_size ** (-0.5)
    visible = (seg_query[:, None] == seg_key[None, :]) & (pos_query[:, None] >= pos_key[None, :])
    masked = jnp.where(visible[None], scores, NEG_FILL)
    new_max = jnp.maximum(run_max, jnp.max(masked, axis=-1))
    weights = jnp.where(visible[None], jnp.exp(masked - new_max[..., None]), 0.0)
    decay = jnp.exp(run_max - new_max)
    run_sum = run_sum * decay + jnp.sum(weights, axis=-1)
    run_acc = run_acc * decay[..., None] + jnp.einsum(
        "htn,nhd->htd", weights, val_part, precision=lax.Precision.HIGHEST
    )
    return (new_max, run_sum, run_acc)


def place_pages(pages, keys_vals, table_row, tok_index):
    rows_here = keys_vals.shape[0]
    blocks_dev = pages.shape[0]
    page_rows = pages.shape[1]
    block_ids = jnp.arange(table_row.shape[0], dtype=jnp.int32)
    wanted = tok_index * blocks_dev + 0
    source = jnp.sum(jnp.where(table_row == wanted, block_ids, 0))
    offset = source * page_rows
    inside = (offset >= 0) & (offset + page_rows <= rows_here)
    block = lax.dynamic_slice_in_dim(
        keys_vals, jnp.clip(offset, 0, rows_here - page_rows), page_rows, 0
    )
    updated = [jnp.where(inside, block, pages[0])]
    return jnp.stack(updated)


def one_layer(
    layer_in, seg_all, table_row, pick_rows, gains, w_qkv, w_out, w_router, w_in, w_down
):
    tok_index = tok_place()
    tok_count = tok_size()
    tok_rows = layer_in.shape[0]
    width = layer_in.shape[1]
    col_width = w_qkv.shape[1] // 3
    head_count = col_width // HEAD_DIM
    experts_all = w_router.shape[1]
    local_pieces = w_in.shape[0]
    split_count = local_pieces * tok_count // experts_all
    blocks_dev = tok_rows // PAGE
    row_ids = jnp.arange(tok_rows, dtype=jnp.int32)
    pos_query = tok_index * tok_rows + row_ids
    seg_query = lax.dynamic_slice_in_dim(seg_all, tok_index * tok_rows, tok_rows)
    resid = layer_in.astype(jnp.float32)
    normed = rms_scale(resid, gains[0]).astype(jnp.bfloat16)
    projected = jnp.dot(normed, w_qkv, preferred_element_type=jnp.float32).astype(jnp.bfloat16)
    projected = projected.reshape(tok_rows, 3, col_width)
    queries = projected[:, 0].reshape(tok_rows, head_count, HEAD_DIM)
    keys_vals = projected[:, 1:]
    soft_init = (
        jnp.full((head_count, tok_rows), NEG_FILL, jnp.float32),
        jnp.zeros((head_count, tok_rows), jnp.float32),
        jnp.zeros((head_count, tok_rows, HEAD_DIM), jnp.float32),
    )
    empty_pages = jnp.zeros((blocks_dev, PAGE, 2, col_width), jnp.bfloat16)
    piece = lax.all_gather(keys_vals, ("tz", "tp"), axis=0, tiled=True)
    rows_key = piece.shape[0]
    window = min(rows_key, -(-(LONGEST + tok_rows) // 256) * 256)
    seg_start = jnp.sum((seg_all < seg_query[0]).astype(jnp.int32))
    window_at = jnp.clip(seg_start, 0, rows_key - window)
    block = lax.dynamic_slice_in_dim(piece, window_at, window, 0)
    seg_key = lax.dynamic_slice_in_dim(seg_all, window_at, window)
    pos_key = window_at + jnp.arange(window, dtype=jnp.int32)
    soft_next = attend(soft_init, queries, block, seg_query, pos_query, seg_key, pos_key)
    pages = place_pages(empty_pages, piece, table_row, tok_index)
    run_max, run_sum, run_acc = soft_next
    context = (
        (run_acc / run_sum[..., None])
        .transpose(1, 0, 2)
        .reshape(tok_rows, col_width)
        .astype(jnp.bfloat16)
    )
    attn_part = jnp.dot(context, w_out, preferred_element_type=jnp.float32)
    mid = resid + rep_sum(attn_part)
    normed_mid = rms_scale(mid, gains[1]).astype(jnp.bfloat16)
    logits = jnp.dot(normed_mid, w_router, preferred_element_type=jnp.float32)
    expert_ids = jnp.arange(experts_all, dtype=jnp.int32)
    chosen = (pick_rows[:, :, None] == expert_ids[None, None, :]).astype(jnp.int32)
    picked_logit = jnp.sum(chosen.astype(jnp.float32) * logits[:, None, :], axis=-1)
    top_logit = jnp.max(picked_logit, axis=-1, keepdims=True)
    raised = jnp.exp(picked_logit - top_logit)
    gate_vals = raised / jnp.sum(raised, axis=-1, keepdims=True)
    ordered = chosen.transpose(1, 0, 2).reshape(TOP * tok_rows, experts_all)
    slot_of = jnp.sum((jnp.cumsum(ordered, axis=0) - 1) * ordered, axis=-1)
    flat_slot = pick_rows.T.reshape(TOP * tok_rows) * CAP + slot_of
    slot_ids = jnp.arange(experts_all * CAP, dtype=jnp.int32)
    hits = (flat_slot[:, None] == slot_ids[None, :]).astype(jnp.int32)
    hits = jnp.sum(hits.reshape(TOP, tok_rows, experts_all * CAP), axis=0).astype(jnp.bfloat16)
    dispatch = lax.dot_general(
        hits, normed_mid, (((0,), (0,)), ((), ())), preferred_element_type=jnp.float32
    ).astype(jnp.bfloat16)
    pair_swap = [(0, 1), (1, 0)]
    own_rows = lax.all_to_all(
        dispatch.reshape(experts_all, CAP, width), "tz", split_axis=0, concat_axis=0, tiled=True
    )
    pair_rows = lax.ppermute(own_rows, "tp", pair_swap)
    rows_all = jnp.stack([own_rows, pair_rows]).reshape(-1, width)
    act = jnp.einsum("rd,dgf->rgf", rows_all, w_in[0], preferred_element_type=jnp.float32)
    hidden = (jax.nn.gelu(act[:, 0, :]) * act[:, 1, :]).astype(jnp.bfloat16)
    share_out = jnp.dot(hidden, w_down[0], preferred_element_type=jnp.float32).astype(jnp.bfloat16)
    share_out = share_out.reshape(2, experts_all, CAP, width)
    pair_out = lax.ppermute(share_out[1], "tp", pair_swap)
    halves = (share_out[0].astype(jnp.float32) + pair_out.astype(jnp.float32)).astype(jnp.bfloat16)
    returned = lax.all_to_all(halves, "tz", split_axis=0, concat_axis=0, tiled=True)
    summed = returned.astype(jnp.float32).reshape(experts_all * CAP, width)
    gathered = jnp.take(summed, flat_slot, axis=0).reshape(TOP, tok_rows, width)
    expert_local = jnp.sum(gate_vals.T[:, :, None] * gathered, axis=0)
    expert_total = rep_sum(expert_local)
    layer_result = (mid + expert_total).astype(jnp.bfloat16)
    return layer_result, pages


def per_device(
    inputs,
    segment_ids,
    picks,
    page_table,
    norm_gains,
    attn_qkv,
    attn_out,
    router,
    expert_in,
    expert_out,
):
    section_index = lax.axis_index("section")
    is_first = section_index == 0
    width = inputs.shape[2]
    own = (
        norm_gains[0],
        attn_qkv[0].reshape(width, -1),
        attn_out[0],
        router[0],
        expert_in[0],
        expert_out[0],
    )
    swap = [(0, 1), (1, 0)]
    other = tuple(lax.ppermute(w, "section", swap) for w in own)
    weights_of = [
        tuple(jnp.where(is_first, a, b) for a, b in zip(own, other)),
        tuple(jnp.where(is_first, b, a) for a, b in zip(own, other)),
    ]
    micro = section_index
    hidden = lax.dynamic_index_in_dim(inputs, micro, 0, keepdims=False)
    seg_all = lax.dynamic_index_in_dim(segment_ids, micro, 0, keepdims=False)
    table_row = lax.dynamic_index_in_dim(page_table, micro, 0, keepdims=False)
    pick_rows = lax.dynamic_index_in_dim(picks, micro, 0, keepdims=False)
    results = []
    for layer in range(2):
        hidden, pages = one_layer(hidden, seg_all, table_row, pick_rows, *weights_of[layer])
        results.append((hidden, pages))
    (res0, pages0), (res1, pages1) = results
    got0 = lax.ppermute(res0, "section", [(1, 0)])
    gotp0 = lax.ppermute(pages0, "section", [(1, 0)])
    got1 = lax.ppermute(res1, "section", [(0, 1)])
    gotp1 = lax.ppermute(pages1, "section", [(0, 1)])
    outputs = jnp.where(is_first, jnp.stack([res0, got0]), jnp.stack([got1, res1]))
    page_out = jnp.where(is_first, jnp.stack([pages0, gotp0]), jnp.stack([gotp1, pages1]))
    return (outputs[None], page_out[None])


def solution(mesh):
    sizes = mesh.shape
    pair = 2
    grid = mesh.devices.reshape(sizes["section"], sizes["tok"] // pair, pair, sizes["rep"])
    split_mesh = Mesh(grid, ("section", "tz", "tp", "rep"))
    tok = ("tz", "tp")
    return jax.shard_map(
        per_device,
        mesh=split_mesh,
        in_specs=(
            P(None, tok, None),
            P(),
            P(None, tok, None),
            P(),
            P("section", None, None),
            P("section", None, None, "rep"),
            P("section", "rep", None),
            P("section", None, None),
            P("section", tok, None, None, "rep"),
            P("section", tok, "rep", None),
        ),
        out_specs=(P("section", None, tok, None), P("section", None, tok, None, None, "rep")),
        check_vma=False,
    )
```

```python
import jax
import jax.numpy as jnp
from jax import lax
from jax.sharding import Mesh, PartitionSpec as P

HEAD_DIM = 64
TOP = 2
PAGE = 128
CAP = 20
LONGEST = 2048


NEG_FILL = -1e30


def shifted(value, axis, steps):
    count = lax.axis_size(axis)
    first, last = (max(0, -steps), min(count, count - steps))
    return lax.ppermute(value, axis, [(source, source + steps) for source in range(first, last)])


def rms_scale(values, gains):
    return values * lax.rsqrt(jnp.mean(values * values, axis=-1, keepdims=True) + 1e-06) * gains


def tok_place():
    return lax.axis_index("tz") * lax.axis_size("tp") + lax.axis_index("tp")


def tok_size():
    return lax.axis_size("tz") * lax.axis_size("tp")


def rep_sum(values):
    count = lax.axis_size("rep")
    own = values.astype(jnp.bfloat16)
    if count != 4:
        return lax.psum(own.astype(jnp.float32), "rep")
    heard = [
        lax.ppermute(own, "rep", [(index, index ^ mask) for index in range(count)]).astype(jnp.float32)
        for mask in (1, 2, 3)
    ]
    return (own.astype(jnp.float32) + heard[0]) + (heard[1] + heard[2])


def attend(carry, queries, keys_vals, seg_query, pos_query, seg_key, pos_key):
    run_max, run_sum, run_acc = carry
    heads_here = run_acc.shape[0]
    head_size = run_acc.shape[2]
    rows_key = keys_vals.shape[0]
    key_part = keys_vals[:, 0].reshape(rows_key, heads_here, head_size)
    val_part = keys_vals[:, 1].reshape(rows_key, heads_here, head_size).astype(jnp.float32)
    scores = jnp.einsum(
        "thd,nhd->htn", queries, key_part, preferred_element_type=jnp.float32
    ) * head_size ** (-0.5)
    visible = (seg_query[:, None] == seg_key[None, :]) & (pos_query[:, None] >= pos_key[None, :])
    masked = jnp.where(visible[None], scores, NEG_FILL)
    new_max = jnp.maximum(run_max, jnp.max(masked, axis=-1))
    weights = jnp.where(visible[None], jnp.exp(masked - new_max[..., None]), 0.0)
    decay = jnp.exp(run_max - new_max)
    run_sum = run_sum * decay + jnp.sum(weights, axis=-1)
    run_acc = run_acc * decay[..., None] + jnp.einsum(
        "htn,nhd->htd", weights, val_part, precision=lax.Precision.HIGHEST
    )
    return (new_max, run_sum, run_acc)


def place_pages(pages, keys_vals, table_row, tok_index):
    rows_here = keys_vals.shape[0]
    blocks_dev = pages.shape[0]
    page_rows = pages.shape[1]
    block_ids = jnp.arange(table_row.shape[0], dtype=jnp.int32)
    wanted = tok_index * blocks_dev + 0
    source = jnp.sum(jnp.where(table_row == wanted, block_ids, 0))
    offset = source * page_rows
    inside = (offset >= 0) & (offset + page_rows <= rows_here)
    block = lax.dynamic_slice_in_dim(
        keys_vals, jnp.clip(offset, 0, rows_here - page_rows), page_rows, 0
    )
    updated = [jnp.where(inside, block, pages[0])]
    return jnp.stack(updated)


def one_layer(
    layer_in, seg_all, table_row, pick_rows, gains, w_qkv, w_out, w_router, w_in, w_down
):
    tok_index = tok_place()
    tok_count = tok_size()
    tok_rows = layer_in.shape[0]
    width = layer_in.shape[1]
    col_width = w_qkv.shape[1] // 3
    head_count = col_width // HEAD_DIM
    experts_all = w_router.shape[1]
    local_pieces = w_in.shape[0]
    split_count = local_pieces * tok_count // experts_all
    blocks_dev = tok_rows // PAGE
    row_ids = jnp.arange(tok_rows, dtype=jnp.int32)
    pos_query = tok_index * tok_rows + row_ids
    seg_query = lax.dynamic_slice_in_dim(seg_all, tok_index * tok_rows, tok_rows)
    resid = layer_in.astype(jnp.float32)
    normed = rms_scale(resid, gains[0]).astype(jnp.bfloat16)
    projected = jnp.dot(normed, w_qkv, preferred_element_type=jnp.float32).astype(jnp.bfloat16)
    projected = projected.reshape(tok_rows, 3, col_width)
    queries = projected[:, 0].reshape(tok_rows, head_count, HEAD_DIM)
    keys_vals = projected[:, 1:]
    soft_init = (
        jnp.full((head_count, tok_rows), NEG_FILL, jnp.float32),
        jnp.zeros((head_count, tok_rows), jnp.float32),
        jnp.zeros((head_count, tok_rows, HEAD_DIM), jnp.float32),
    )
    empty_pages = jnp.zeros((blocks_dev, PAGE, 2, col_width), jnp.bfloat16)
    piece = lax.all_gather(keys_vals, ("tz", "tp"), axis=0, tiled=True)
    rows_key = piece.shape[0]
    window = min(rows_key, -(-(LONGEST + tok_rows) // 256) * 256)
    seg_start = jnp.sum((seg_all < seg_query[0]).astype(jnp.int32))
    window_at = jnp.clip(seg_start, 0, rows_key - window)
    block = lax.dynamic_slice_in_dim(piece, window_at, window, 0)
    seg_key = lax.dynamic_slice_in_dim(seg_all, window_at, window)
    pos_key = window_at + jnp.arange(window, dtype=jnp.int32)
    soft_next = attend(soft_init, queries, block, seg_query, pos_query, seg_key, pos_key)
    pages = place_pages(empty_pages, piece, table_row, tok_index)
    run_max, run_sum, run_acc = soft_next
    context = (
        (run_acc / run_sum[..., None])
        .transpose(1, 0, 2)
        .reshape(tok_rows, col_width)
        .astype(jnp.bfloat16)
    )
    attn_part = jnp.dot(context, w_out, preferred_element_type=jnp.float32)
    mid = resid + rep_sum(attn_part)
    normed_mid = rms_scale(mid, gains[1]).astype(jnp.bfloat16)
    logits = jnp.dot(normed_mid, w_router, preferred_element_type=jnp.float32)
    expert_ids = jnp.arange(experts_all, dtype=jnp.int32)
    chosen = (pick_rows[:, :, None] == expert_ids[None, None, :]).astype(jnp.int32)
    picked_logit = jnp.sum(chosen.astype(jnp.float32) * logits[:, None, :], axis=-1)
    top_logit = jnp.max(picked_logit, axis=-1, keepdims=True)
    raised = jnp.exp(picked_logit - top_logit)
    gate_vals = raised / jnp.sum(raised, axis=-1, keepdims=True)
    ordered = chosen.transpose(1, 0, 2).reshape(TOP * tok_rows, experts_all)
    slot_of = jnp.sum((jnp.cumsum(ordered, axis=0) - 1) * ordered, axis=-1)
    flat_slot = pick_rows.T.reshape(TOP * tok_rows) * CAP + slot_of
    slot_ids = jnp.arange(experts_all * CAP, dtype=jnp.int32)
    hits = (flat_slot[:, None] == slot_ids[None, :]).astype(jnp.int32)
    hits = jnp.sum(hits.reshape(TOP, tok_rows, experts_all * CAP), axis=0).astype(jnp.bfloat16)
    dispatch = lax.dot_general(
        hits, normed_mid, (((0,), (0,)), ((), ())), preferred_element_type=jnp.float32
    ).astype(jnp.bfloat16)
    pair_swap = [(0, 1), (1, 0)]
    own_rows = lax.all_to_all(
        dispatch.reshape(experts_all, CAP, width), "tz", split_axis=0, concat_axis=0, tiled=True
    )
    pair_rows = lax.ppermute(own_rows, "tp", pair_swap)
    rows_all = jnp.stack([own_rows, pair_rows]).reshape(-1, width)
    act = jnp.einsum("rd,dgf->rgf", rows_all, w_in[0], preferred_element_type=jnp.float32)
    hidden = (jax.nn.gelu(act[:, 0, :]) * act[:, 1, :]).astype(jnp.bfloat16)
    share_out = jnp.dot(hidden, w_down[0], preferred_element_type=jnp.float32).astype(jnp.bfloat16)
    share_out = share_out.reshape(2, experts_all, CAP, width)
    pair_out = lax.ppermute(share_out[1], "tp", pair_swap)
    halves = (share_out[0].astype(jnp.float32) + pair_out.astype(jnp.float32)).astype(jnp.bfloat16)
    returned = lax.all_to_all(halves, "tz", split_axis=0, concat_axis=0, tiled=True)
    summed = returned.astype(jnp.float32).reshape(experts_all * CAP, width)
    gathered = jnp.take(summed, flat_slot, axis=0).reshape(TOP, tok_rows, width)
    expert_local = jnp.sum(gate_vals.T[:, :, None] * gathered, axis=0)
    expert_total = rep_sum(expert_local)
    layer_result = (mid + expert_total).astype(jnp.bfloat16)
    return layer_result, pages


def per_device(
    inputs,
    segment_ids,
    picks,
    page_table,
    norm_gains,
    attn_qkv,
    attn_out,
    router,
    expert_in,
    expert_out,
):
    section_index = lax.axis_index("section")
    is_first = section_index == 0
    width = inputs.shape[2]
    own = (
        norm_gains[0],
        attn_qkv[0].reshape(width, -1),
        attn_out[0],
        router[0],
        expert_in[0],
        expert_out[0],
    )
    swap = [(0, 1), (1, 0)]
    other = tuple(lax.ppermute(w, "section", swap) for w in own)
    weights_of = [
        tuple(jnp.where(is_first, a, b) for a, b in zip(own, other)),
        tuple(jnp.where(is_first, b, a) for a, b in zip(own, other)),
    ]
    micro = section_index
    hidden = lax.dynamic_index_in_dim(inputs, micro, 0, keepdims=False)
    seg_all = lax.dynamic_index_in_dim(segment_ids, micro, 0, keepdims=False)
    table_row = lax.dynamic_index_in_dim(page_table, micro, 0, keepdims=False)
    pick_rows = lax.dynamic_index_in_dim(picks, micro, 0, keepdims=False)
    results = []
    for layer in range(2):
        hidden, pages = one_layer(hidden, seg_all, table_row, pick_rows, *weights_of[layer])
        results.append((hidden, pages))
    (res0, pages0), (res1, pages1) = results
    got0 = lax.ppermute(res0, "section", [(1, 0)])
    gotp0 = lax.ppermute(pages0, "section", [(1, 0)])
    got1 = lax.ppermute(res1, "section", [(0, 1)])
    gotp1 = lax.ppermute(pages1, "section", [(0, 1)])
    outputs = jnp.where(is_first, jnp.stack([res0, got0]), jnp.stack([got1, res1]))
    page_out = jnp.where(is_first, jnp.stack([pages0, gotp0]), jnp.stack([gotp1, pages1]))
    return (outputs[None], page_out[None])


def solution(mesh):
    sizes = mesh.shape
    pair = 2
    grid = mesh.devices.reshape(sizes["section"], sizes["tok"] // pair, pair, sizes["rep"])
    split_mesh = Mesh(grid, ("section", "tz", "tp", "rep"))
    tok = ("tz", "tp")
    return jax.shard_map(
        per_device,
        mesh=split_mesh,
        in_specs=(
            P(None, tok, None),
            P(),
            P(None, tok, None),
            P(),
            P("section", None, None),
            P("section", None, None, "rep"),
            P("section", "rep", None),
            P("section", None, None),
            P("section", tok, None, None, "rep"),
            P("section", tok, "rep", None),
        ),
        out_specs=(P("section", None, tok, None), P("section", None, tok, None, None, "rep")),
        check_vma=False,
    )
```

```python
import jax
import jax.numpy as jnp
from jax import lax
from jax.sharding import Mesh, PartitionSpec as P

HEAD_DIM = 64
TOP = 2
PAGE = 128
CAP = 20
LONGEST = 2048


NEG_FILL = -1e30


def shifted(value, axis, steps):
    count = lax.axis_size(axis)
    first, last = (max(0, -steps), min(count, count - steps))
    return lax.ppermute(value, axis, [(source, source + steps) for source in range(first, last)])


def rms_scale(values, gains):
    return values * lax.rsqrt(jnp.mean(values * values, axis=-1, keepdims=True) + 1e-06) * gains


def tok_place():
    return lax.axis_index("tz") * lax.axis_size("tp") + lax.axis_index("tp")


def tok_size():
    return lax.axis_size("tz") * lax.axis_size("tp")


def rep_sum(values):
    count = lax.axis_size("rep")
    own = values.astype(jnp.bfloat16)
    if count != 4:
        return lax.psum(own.astype(jnp.float32), "rep")
    heard = [
        lax.ppermute(own, "rep", [(index, index ^ mask) for index in range(count)]).astype(jnp.float32)
        for mask in (1, 2, 3)
    ]
    return (own.astype(jnp.float32) + heard[0]) + (heard[1] + heard[2])


def attend(carry, queries, keys_vals, seg_query, pos_query, seg_key, pos_key):
    run_max, run_sum, run_acc = carry
    heads_here = run_acc.shape[0]
    head_size = run_acc.shape[2]
    rows_key = keys_vals.shape[0]
    key_part = keys_vals[:, 0].reshape(rows_key, heads_here, head_size)
    val_part = keys_vals[:, 1].reshape(rows_key, heads_here, head_size).astype(jnp.float32)
    scores = jnp.einsum(
        "thd,nhd->htn", queries, key_part, preferred_element_type=jnp.float32
    ) * head_size ** (-0.5)
    visible = (seg_query[:, None] == seg_key[None, :]) & (pos_query[:, None] >= pos_key[None, :])
    masked = jnp.where(visible[None], scores, NEG_FILL)
    new_max = jnp.maximum(run_max, jnp.max(masked, axis=-1))
    weights = jnp.where(visible[None], jnp.exp(masked - new_max[..., None]), 0.0)
    decay = jnp.exp(run_max - new_max)
    run_sum = run_sum * decay + jnp.sum(weights, axis=-1)
    run_acc = run_acc * decay[..., None] + jnp.einsum(
        "htn,nhd->htd", weights, val_part, precision=lax.Precision.HIGHEST
    )
    return (new_max, run_sum, run_acc)


def place_pages(pages, keys_vals, table_row, tok_index):
    rows_here = keys_vals.shape[0]
    blocks_dev = pages.shape[0]
    page_rows = pages.shape[1]
    block_ids = jnp.arange(table_row.shape[0], dtype=jnp.int32)
    wanted = tok_index * blocks_dev + 0
    source = jnp.sum(jnp.where(table_row == wanted, block_ids, 0))
    offset = source * page_rows
    inside = (offset >= 0) & (offset + page_rows <= rows_here)
    block = lax.dynamic_slice_in_dim(
        keys_vals, jnp.clip(offset, 0, rows_here - page_rows), page_rows, 0
    )
    updated = [jnp.where(inside, block, pages[0])]
    return jnp.stack(updated)


def one_layer(
    layer_in, seg_all, table_row, pick_rows, gains, w_qkv, w_out, w_router, w_in, w_down
):
    tok_index = tok_place()
    tok_count = tok_size()
    tok_rows = layer_in.shape[0]
    width = layer_in.shape[1]
    col_width = w_qkv.shape[1] // 3
    head_count = col_width // HEAD_DIM
    experts_all = w_router.shape[1]
    local_pieces = w_in.shape[0]
    split_count = local_pieces * tok_count // experts_all
    blocks_dev = tok_rows // PAGE
    row_ids = jnp.arange(tok_rows, dtype=jnp.int32)
    pos_query = tok_index * tok_rows + row_ids
    seg_query = lax.dynamic_slice_in_dim(seg_all, tok_index * tok_rows, tok_rows)
    resid = layer_in.astype(jnp.float32)
    normed = rms_scale(resid, gains[0]).astype(jnp.bfloat16)
    projected = jnp.dot(normed, w_qkv, preferred_element_type=jnp.float32).astype(jnp.bfloat16)
    projected = projected.reshape(tok_rows, 3, col_width)
    queries = projected[:, 0].reshape(tok_rows, head_count, HEAD_DIM)
    keys_vals = projected[:, 1:]
    soft_init = (
        jnp.full((head_count, tok_rows), NEG_FILL, jnp.float32),
        jnp.zeros((head_count, tok_rows), jnp.float32),
        jnp.zeros((head_count, tok_rows, HEAD_DIM), jnp.float32),
    )
    empty_pages = jnp.zeros((blocks_dev, PAGE, 2, col_width), jnp.bfloat16)
    piece = lax.all_gather(keys_vals, ("tz", "tp"), axis=0, tiled=True)
    rows_key = piece.shape[0]
    window = min(rows_key, -(-(LONGEST + tok_rows) // 256) * 256)
    seg_start = jnp.sum((seg_all < seg_query[0]).astype(jnp.int32))
    window_at = jnp.clip(seg_start, 0, rows_key - window)
    block = lax.dynamic_slice_in_dim(piece, window_at, window, 0)
    seg_key = lax.dynamic_slice_in_dim(seg_all, window_at, window)
    pos_key = window_at + jnp.arange(window, dtype=jnp.int32)
    soft_next = attend(soft_init, queries, block, seg_query, pos_query, seg_key, pos_key)
    pages = place_pages(empty_pages, piece, table_row, tok_index)
    run_max, run_sum, run_acc = soft_next
    context = (
        (run_acc / run_sum[..., None])
        .transpose(1, 0, 2)
        .reshape(tok_rows, col_width)
        .astype(jnp.bfloat16)
    )
    attn_part = jnp.dot(context, w_out, preferred_element_type=jnp.float32)
    mid = resid + rep_sum(attn_part)
    normed_mid = rms_scale(mid, gains[1]).astype(jnp.bfloat16)
    logits = jnp.dot(normed_mid, w_router, preferred_element_type=jnp.float32)
    expert_ids = jnp.arange(experts_all, dtype=jnp.int32)
    chosen = (pick_rows[:, :, None] == expert_ids[None, None, :]).astype(jnp.int32)
    picked_logit = jnp.sum(chosen.astype(jnp.float32) * logits[:, None, :], axis=-1)
    top_logit = jnp.max(picked_logit, axis=-1, keepdims=True)
    raised = jnp.exp(picked_logit - top_logit)
    gate_vals = raised / jnp.sum(raised, axis=-1, keepdims=True)
    ordered = chosen.transpose(1, 0, 2).reshape(TOP * tok_rows, experts_all)
    slot_of = jnp.sum((jnp.cumsum(ordered, axis=0) - 1) * ordered, axis=-1)
    flat_slot = pick_rows.T.reshape(TOP * tok_rows) * CAP + slot_of
    slot_ids = jnp.arange(experts_all * CAP, dtype=jnp.int32)
    hits = (flat_slot[:, None] == slot_ids[None, :]).astype(jnp.int32)
    hits = jnp.sum(hits.reshape(TOP, tok_rows, experts_all * CAP), axis=0).astype(jnp.bfloat16)
    dispatch = lax.dot_general(
        hits, normed_mid, (((0,), (0,)), ((), ())), preferred_element_type=jnp.float32
    ).astype(jnp.bfloat16)
    pair_swap = [(0, 1), (1, 0)]
    own_rows = lax.all_to_all(
        dispatch.reshape(experts_all, CAP, width), "tz", split_axis=0, concat_axis=0, tiled=True
    )
    pair_rows = lax.ppermute(own_rows, "tp", pair_swap)
    rows_all = jnp.stack([own_rows, pair_rows]).reshape(-1, width)
    act = jnp.einsum("rd,dgf->rgf", rows_all, w_in[0], preferred_element_type=jnp.float32)
    hidden = (jax.nn.gelu(act[:, 0, :]) * act[:, 1, :]).astype(jnp.bfloat16)
    share_out = jnp.dot(hidden, w_down[0], preferred_element_type=jnp.float32).astype(jnp.bfloat16)
    share_out = share_out.reshape(2, experts_all, CAP, width)
    pair_out = lax.ppermute(share_out[1], "tp", pair_swap)
    halves = (share_out[0].astype(jnp.float32) + pair_out.astype(jnp.float32)).astype(jnp.bfloat16)
    returned = lax.all_to_all(halves, "tz", split_axis=0, concat_axis=0, tiled=True)
    summed = returned.astype(jnp.float32).reshape(experts_all * CAP, width)
    gathered = jnp.take(summed, flat_slot, axis=0).reshape(TOP, tok_rows, width)
    expert_local = jnp.sum(gate_vals.T[:, :, None] * gathered, axis=0)
    expert_total = rep_sum(expert_local)
    layer_result = (mid + expert_total).astype(jnp.bfloat16)
    return layer_result, pages


def per_device(
    inputs,
    segment_ids,
    picks,
    page_table,
    norm_gains,
    attn_qkv,
    attn_out,
    router,
    expert_in,
    expert_out,
):
    section_index = lax.axis_index("section")
    is_first = section_index == 0
    width = inputs.shape[2]
    own = (
        norm_gains[0],
        attn_qkv[0].reshape(width, -1),
        attn_out[0],
        router[0],
        expert_in[0],
        expert_out[0],
    )
    swap = [(0, 1), (1, 0)]
    other = tuple(lax.ppermute(w, "section", swap) for w in own)
    weights_of = [
        tuple(jnp.where(is_first, a, b) for a, b in zip(own, other)),
        tuple(jnp.where(is_first, b, a) for a, b in zip(own, other)),
    ]
    micro = section_index
    hidden = lax.dynamic_index_in_dim(inputs, micro, 0, keepdims=False)
    seg_all = lax.dynamic_index_in_dim(segment_ids, micro, 0, keepdims=False)
    table_row = lax.dynamic_index_in_dim(page_table, micro, 0, keepdims=False)
    pick_rows = lax.dynamic_index_in_dim(picks, micro, 0, keepdims=False)
    stacked = tuple(jnp.stack([first, second]) for first, second in zip(*weights_of))
    res_init = jnp.zeros((2,) + hidden.shape, hidden.dtype)
    blocks_dev = hidden.shape[0] // PAGE
    page_init = jnp.zeros((2, blocks_dev, PAGE, 2, stacked[1].shape[2] // 3), jnp.bfloat16)

    def layer_step(layer, carry):
        now, res_all, page_all = carry
        chosen = tuple(lax.dynamic_index_in_dim(w, layer, 0, keepdims=False) for w in stacked)
        now, pages = one_layer(now, seg_all, table_row, pick_rows, *chosen)
        res_all = lax.dynamic_update_index_in_dim(res_all, now, layer, 0)
        page_all = lax.dynamic_update_index_in_dim(page_all, pages, layer, 0)
        return now, res_all, page_all

    _, res_all, page_all = lax.fori_loop(0, 2, layer_step, (hidden, res_init, page_init))
    res0, res1 = res_all[0], res_all[1]
    pages0, pages1 = page_all[0], page_all[1]
    got0 = lax.ppermute(res0, "section", [(1, 0)])
    gotp0 = lax.ppermute(pages0, "section", [(1, 0)])
    got1 = lax.ppermute(res1, "section", [(0, 1)])
    gotp1 = lax.ppermute(pages1, "section", [(0, 1)])
    outputs = jnp.where(is_first, jnp.stack([res0, got0]), jnp.stack([got1, res1]))
    page_out = jnp.where(is_first, jnp.stack([pages0, gotp0]), jnp.stack([gotp1, pages1]))
    return (outputs[None], page_out[None])


def solution(mesh):
    sizes = mesh.shape
    pair = 2
    grid = mesh.devices.reshape(sizes["section"], sizes["tok"] // pair, pair, sizes["rep"])
    split_mesh = Mesh(grid, ("section", "tz", "tp", "rep"))
    tok = ("tz", "tp")
    return jax.shard_map(
        per_device,
        mesh=split_mesh,
        in_specs=(
            P(None, tok, None),
            P(),
            P(None, tok, None),
            P(),
            P("section", None, None),
            P("section", None, None, "rep"),
            P("section", "rep", None),
            P("section", None, None),
            P("section", tok, None, None, "rep"),
            P("section", tok, "rep", None),
        ),
        out_specs=(P("section", None, tok, None), P("section", None, tok, None, None, "rep")),
        check_vma=False,
    )
```

```python
import jax
import jax.numpy as jnp
from jax import lax
from jax.sharding import Mesh, PartitionSpec as P

HEAD_DIM = 64
TOP = 2
PAGE = 128
CAP = 20
LONGEST = 2048


NEG_FILL = -1e30


def shifted(value, axis, steps):
    count = lax.axis_size(axis)
    first, last = (max(0, -steps), min(count, count - steps))
    return lax.ppermute(value, axis, [(source, source + steps) for source in range(first, last)])


def rms_scale(values, gains):
    return values * lax.rsqrt(jnp.mean(values * values, axis=-1, keepdims=True) + 1e-06) * gains


def tok_place():
    return lax.axis_index("tz") * lax.axis_size("tp") + lax.axis_index("tp")


def tok_size():
    return lax.axis_size("tz") * lax.axis_size("tp")


def rep_sum(values):
    count = lax.axis_size("rep")
    own = values.astype(jnp.bfloat16)
    if count != 4:
        return lax.psum(own.astype(jnp.float32), "rep")
    heard = [
        lax.ppermute(own, "rep", [(index, index ^ mask) for index in range(count)]).astype(jnp.float32)
        for mask in (1, 2, 3)
    ]
    return (own.astype(jnp.float32) + heard[0]) + (heard[1] + heard[2])


def attend(carry, queries, keys_vals, seg_query, pos_query, seg_key, pos_key):
    run_max, run_sum, run_acc = carry
    heads_here = run_acc.shape[0]
    head_size = run_acc.shape[2]
    rows_key = keys_vals.shape[0]
    key_part = keys_vals[:, 0].reshape(rows_key, heads_here, head_size)
    val_part = keys_vals[:, 1].reshape(rows_key, heads_here, head_size).astype(jnp.float32)
    scores = jnp.einsum(
        "thd,nhd->htn", queries, key_part, preferred_element_type=jnp.float32
    ) * head_size ** (-0.5)
    visible = (seg_query[:, None] == seg_key[None, :]) & (pos_query[:, None] >= pos_key[None, :])
    masked = jnp.where(visible[None], scores, NEG_FILL)
    new_max = jnp.maximum(run_max, jnp.max(masked, axis=-1))
    weights = jnp.where(visible[None], jnp.exp(masked - new_max[..., None]), 0.0)
    decay = jnp.exp(run_max - new_max)
    run_sum = run_sum * decay + jnp.sum(weights, axis=-1)
    run_acc = run_acc * decay[..., None] + jnp.einsum(
        "htn,nhd->htd", weights, val_part, precision=lax.Precision.HIGHEST
    )
    return (new_max, run_sum, run_acc)


def place_pages(pages, keys_vals, table_row, tok_index):
    rows_here = keys_vals.shape[0]
    blocks_dev = pages.shape[0]
    page_rows = pages.shape[1]
    block_ids = jnp.arange(table_row.shape[0], dtype=jnp.int32)
    wanted = tok_index * blocks_dev + 0
    source = jnp.sum(jnp.where(table_row == wanted, block_ids, 0))
    offset = source * page_rows
    inside = (offset >= 0) & (offset + page_rows <= rows_here)
    block = lax.dynamic_slice_in_dim(
        keys_vals, jnp.clip(offset, 0, rows_here - page_rows), page_rows, 0
    )
    updated = [jnp.where(inside, block, pages[0])]
    return jnp.stack(updated)


def one_layer(
    layer_in, seg_all, table_row, pick_rows, gains, w_qkv, w_out, w_router, w_in, w_down
):
    tok_index = tok_place()
    tok_count = tok_size()
    tok_rows = layer_in.shape[0]
    width = layer_in.shape[1]
    col_width = w_qkv.shape[1] // 3
    head_count = col_width // HEAD_DIM
    experts_all = w_router.shape[1]
    local_pieces = w_in.shape[0]
    split_count = local_pieces * tok_count // experts_all
    blocks_dev = tok_rows // PAGE
    row_ids = jnp.arange(tok_rows, dtype=jnp.int32)
    pos_query = tok_index * tok_rows + row_ids
    seg_query = lax.dynamic_slice_in_dim(seg_all, tok_index * tok_rows, tok_rows)
    resid = layer_in.astype(jnp.float32)
    normed = rms_scale(resid, gains[0]).astype(jnp.bfloat16)
    projected = jnp.dot(normed, w_qkv, preferred_element_type=jnp.float32).astype(jnp.bfloat16)
    projected = projected.reshape(tok_rows, 3, col_width)
    queries = projected[:, 0].reshape(tok_rows, head_count, HEAD_DIM)
    keys_vals = projected[:, 1:]
    soft_init = (
        jnp.full((head_count, tok_rows), NEG_FILL, jnp.float32),
        jnp.zeros((head_count, tok_rows), jnp.float32),
        jnp.zeros((head_count, tok_rows, HEAD_DIM), jnp.float32),
    )
    empty_pages = jnp.zeros((blocks_dev, PAGE, 2, col_width), jnp.bfloat16)
    piece = lax.all_gather(keys_vals, ("tz", "tp"), axis=0, tiled=True)
    rows_key = piece.shape[0]
    window = min(rows_key, -(-(LONGEST + tok_rows) // 256) * 256)
    seg_start = jnp.sum((seg_all < seg_query[0]).astype(jnp.int32))
    window_at = jnp.clip(seg_start, 0, rows_key - window)
    block = lax.dynamic_slice_in_dim(piece, window_at, window, 0)
    seg_key = lax.dynamic_slice_in_dim(seg_all, window_at, window)
    pos_key = window_at + jnp.arange(window, dtype=jnp.int32)
    soft_next = attend(soft_init, queries, block, seg_query, pos_query, seg_key, pos_key)
    pages = place_pages(empty_pages, piece, table_row, tok_index)
    run_max, run_sum, run_acc = soft_next
    context = (
        (run_acc / run_sum[..., None])
        .transpose(1, 0, 2)
        .reshape(tok_rows, col_width)
        .astype(jnp.bfloat16)
    )
    attn_part = jnp.dot(context, w_out, preferred_element_type=jnp.float32)
    mid = resid + rep_sum(attn_part)
    normed_mid = rms_scale(mid, gains[1]).astype(jnp.bfloat16)
    logits = jnp.dot(normed_mid, w_router, preferred_element_type=jnp.float32)
    expert_ids = jnp.arange(experts_all, dtype=jnp.int32)
    chosen = (pick_rows[:, :, None] == expert_ids[None, None, :]).astype(jnp.int32)
    picked_logit = jnp.sum(chosen.astype(jnp.float32) * logits[:, None, :], axis=-1)
    top_logit = jnp.max(picked_logit, axis=-1, keepdims=True)
    raised = jnp.exp(picked_logit - top_logit)
    gate_vals = raised / jnp.sum(raised, axis=-1, keepdims=True)
    ordered = chosen.transpose(1, 0, 2).reshape(TOP * tok_rows, experts_all)
    slot_of = jnp.sum((jnp.cumsum(ordered, axis=0) - 1) * ordered, axis=-1)
    flat_slot = pick_rows.T.reshape(TOP * tok_rows) * CAP + slot_of
    slot_ids = jnp.arange(experts_all * CAP, dtype=jnp.int32)
    hits = (flat_slot[:, None] == slot_ids[None, :]).astype(jnp.int32)
    hits = jnp.sum(hits.reshape(TOP, tok_rows, experts_all * CAP), axis=0).astype(jnp.bfloat16)
    dispatch = lax.dot_general(
        hits, normed_mid, (((0,), (0,)), ((), ())), preferred_element_type=jnp.float32
    ).astype(jnp.bfloat16)
    pair_swap = [(0, 1), (1, 0)]
    own_rows = lax.all_to_all(
        dispatch.reshape(experts_all, CAP, width), "tz", split_axis=0, concat_axis=0, tiled=True
    )
    pair_rows = lax.ppermute(own_rows, "tp", pair_swap)
    rows_all = jnp.stack([own_rows, pair_rows]).reshape(-1, width)
    act = jnp.einsum("rd,dgf->rgf", rows_all, w_in[0], preferred_element_type=jnp.float32)
    hidden = (jax.nn.gelu(act[:, 0, :]) * act[:, 1, :]).astype(jnp.bfloat16)
    share_out = jnp.dot(hidden, w_down[0], preferred_element_type=jnp.float32).astype(jnp.bfloat16)
    share_out = share_out.reshape(2, experts_all, CAP, width)
    pair_out = lax.ppermute(share_out[1], "tp", pair_swap)
    halves = (share_out[0].astype(jnp.float32) + pair_out.astype(jnp.float32)).astype(jnp.bfloat16)
    returned = lax.all_to_all(halves, "tz", split_axis=0, concat_axis=0, tiled=True)
    summed = returned.astype(jnp.float32).reshape(experts_all * CAP, width)
    gathered = jnp.take(summed, flat_slot, axis=0).reshape(TOP, tok_rows, width)
    expert_local = jnp.sum(gate_vals.T[:, :, None] * gathered, axis=0)
    expert_total = rep_sum(expert_local)
    layer_result = (mid + expert_total).astype(jnp.bfloat16)
    return layer_result, pages


def per_device(
    inputs,
    segment_ids,
    picks,
    page_table,
    norm_gains,
    attn_qkv,
    attn_out,
    router,
    expert_in,
    expert_out,
):
    section_index = lax.axis_index("section")
    is_first = section_index == 0
    width = inputs.shape[2]
    own = (
        norm_gains[0],
        attn_qkv[0].reshape(width, -1),
        attn_out[0],
        router[0],
        expert_in[0],
        expert_out[0],
    )
    swap = [(0, 1), (1, 0)]
    other = tuple(lax.ppermute(w, "section", swap) for w in own)
    weights_of = [
        tuple(jnp.where(is_first, a, b) for a, b in zip(own, other)),
        tuple(jnp.where(is_first, b, a) for a, b in zip(own, other)),
    ]
    micro = section_index
    hidden = lax.dynamic_index_in_dim(inputs, micro, 0, keepdims=False)
    seg_all = lax.dynamic_index_in_dim(segment_ids, micro, 0, keepdims=False)
    table_row = lax.dynamic_index_in_dim(page_table, micro, 0, keepdims=False)
    pick_rows = lax.dynamic_index_in_dim(picks, micro, 0, keepdims=False)
    results = []
    for layer in range(2):
        hidden, pages = one_layer(hidden, seg_all, table_row, pick_rows, *weights_of[layer])
        results.append((hidden, pages))
    (res0, pages0), (res1, pages1) = results
    def packed_send(res, pages, pairs):
        flat = jnp.concatenate([res.reshape(-1), pages.reshape(-1)])
        got = lax.ppermute(flat, "section", pairs)
        return got[: res.size].reshape(res.shape), got[res.size :].reshape(pages.shape)

    got0, gotp0 = packed_send(res0, pages0, [(1, 0)])
    got1, gotp1 = packed_send(res1, pages1, [(0, 1)])
    outputs = jnp.where(is_first, jnp.stack([res0, got0]), jnp.stack([got1, res1]))
    page_out = jnp.where(is_first, jnp.stack([pages0, gotp0]), jnp.stack([gotp1, pages1]))
    return (outputs[None], page_out[None])


def solution(mesh):
    sizes = mesh.shape
    pair = 2
    grid = mesh.devices.reshape(sizes["section"], sizes["tok"] // pair, pair, sizes["rep"])
    split_mesh = Mesh(grid, ("section", "tz", "tp", "rep"))
    tok = ("tz", "tp")
    return jax.shard_map(
        per_device,
        mesh=split_mesh,
        in_specs=(
            P(None, tok, None),
            P(),
            P(None, tok, None),
            P(),
            P("section", None, None),
            P("section", None, None, "rep"),
            P("section", "rep", None),
            P("section", None, None),
            P("section", tok, None, None, "rep"),
            P("section", tok, "rep", None),
        ),
        out_specs=(P("section", None, tok, None), P("section", None, tok, None, None, "rep")),
        check_vma=False,
    )
```
